128 devices in a mesh: seq: 16 (over y, x), batch: 8 (over z, core).
Axes of the slice: x: 4, y: 4, z: 4, core: 2. Of those that a mesh axis runs over, the one named last changes fastest.
Arguments:
- ssm_input: bfloat16 [32768, 4096], P(('batch', 'seq')), parts along dimension 0, may hold values from -6 to 6
- gate_input: bfloat16 [32768, 4096], P(('batch', 'seq')), parts along dimension 0, may hold values from -6 to 6
- b_rows: bfloat16 [32768, 128], P(('batch', 'seq')), parts along dimension 0, may hold values from -6 to 6
- c_rows: bfloat16 [32768, 128], P(('batch', 'seq')), parts along dimension 0, may hold values from -6 to 6
- step_raw: float32 [32768, 64], P(('batch', 'seq')), parts along dimension 0, may hold values from -14 to 2
- step_bias: float32 [64], replicated, may hold values from -0.5 to 0.5
- rate_log: float32 [64], replicated, may hold values from -1.5 to 4
- skip_gain: float32 [64], replicated, may hold values from 0.5 to 2
- norm_gain: float32 [4096], replicated, may hold values from 0.5 to 1.5
- w_out: bfloat16 [4096, 4096], P(None, 'seq'), may hold values from -0.09375 to 0.09375
- residual: bfloat16 [32768, 4096], P(('batch', 'seq')), parts along dimension 0, may hold values from -6 to 6
- moe_gain: float32 [4096], replicated, may hold values from 0.5 to 1.5
- router: bfloat16 [4096, 16], replicated, may hold values from -0.09375 to 0.09375
- expert_ids: int32 [32768, 2], P(('batch', 'seq')), parts along dimension 0, may hold values from 0 to 15, all different within a row; in each aligned block of 256 rows (0 to 255, 256 to 511, ...) at most 48 rows name the same one
- w_gate: bfloat16 [16, 4096, 384], P('seq'), may hold values from -0.09375 to 0.09375
- w_up: bfloat16 [16, 4096, 384], P('seq'), may hold values from -0.09375 to 0.09375
- w_down: bfloat16 [16, 384, 4096], P('seq'), may hold values from -0.3125 to 0.3125
Outputs:
- layer_out: bfloat16 [32768, 4096], P(('batch', 'seq')), parts along dimension 0
The draws below stay inside these ranges and needn't reach their ends.
There are 8 independent parts, one for each index of `batch`. The reference program is written for one: setup_inputs(seed, part) draws one part's arguments, and reference() takes and returns one part's arrays. A program takes and returns all parts, laid end to end along the dimension named above; an argument that names none is the same for every part. Nothing has to cross between parts.
Inputs may be any that keep to these rules, and one draw needn't show every extreme that they name: `expert_ids`: the 2 ids of a token differ. In the rows of one device (256 rows, aligned blocks), no expert is named by more than 48 rows, a bound that some block reaches.
All inputs are finite; a program needn't handle non-finite values.
Results may differ from the reference program's by a relative error of at most 0.008.
Values may be sent and summed in bfloat16 or wider, within the bound.
No kernel may reach another device: no remote copies, remote signals or barrier semaphores. Data moves between devices by JAX's collectives and lax.ppermute only.
A program may use at most 192 MiB of HBM per device.

```python
import math
import jax
import jax.numpy as jnp
import numpy as np
from jax import lax

D = 4096
HEADS = 64
HEAD_DIM = 64
STATE = 128
D_IN = 4096
FF = 384
TOP = 2
GROUP = 256
TOK_DEV = 256
LEN = 4096
EXPERTS = 16
CAP = 48
N_SEQ = 16


def draw_rate_log(key, part):
    first, second, third = jax.random.split(key, 3)
    fast = jax.random.bernoulli(first, 0.5, (HEADS,))
    slow_rate = jnp.exp(jax.random.uniform(second, (HEADS,), jnp.float32, math.log(0.25), math.log(0.45)))
    fast_rate = LEN / 3.0 * jnp.exp(jax.random.uniform(third, (HEADS,), jnp.float32, math.log(1.0 / 50.0), math.log(1.0 / 30.0)))
    chosen = jnp.log(jnp.where(fast, fast_rate, slow_rate))
    return jnp.minimum(chosen, 4.0).astype(jnp.float32)


def draw_step_raw(key, part):
    first, second, third, fourth = jax.random.split(key, 4)
    noise = 0.4 * jax.random.normal(first, (LEN, HEADS), jnp.float32)
    slabs = jax.random.uniform(second, (LEN // TOK_DEV, HEADS), jnp.float32, -0.6, 0.6)
    slab_shift = jnp.repeat(slabs, TOK_DEV, axis=0)
    starting_offset = math.log(3.0 / LEN) + noise + slab_shift
    expert_slot_positions = jax.random.randint(third, (2,), 0, LEN)
    position_indices = jnp.arange(LEN)
    token_group_size = jnp.any(position_indices[:, None] == expert_slot_positions[None, :], axis=1)
    doubling_depth = jax.random.uniform(fourth, (LEN, HEADS), jnp.float32, 0.0, 1.1)
    return jnp.where(token_group_size[:, None], doubling_depth, starting_offset).astype(jnp.float32)


def block_levels(stream_key, dims, cuts, low, top_value):
    level, own = 1.0, jax.random.fold_in(stream_key, 6)
    for axis_at, parts in cuts:
        draws = jnp.exp(jax.random.uniform(jax.random.fold_in(own, axis_at), (parts,), jnp.float32, low / len(cuts), top_value / len(cuts)))
        level = level * jnp.repeat(draws, dims[axis_at] // parts).reshape([-1 if axis == axis_at else 1 for axis in range(len(dims))])
    return level


def shared_out(stream_key, own, number, rows, amount, top, bound, skew):
    ranking = jax.random.permutation(stream_key, amount)
    heavy_load, usual = load_shares(amount, rows * top, bound, skew, True), load_shares(amount, rows * top, bound, skew, False)
    places = jnp.arange(amount)

    def named(sizes, offset_by):
        used = int((sizes > 0).sum())
        fixed = max(1, used // 4)
        moved = fixed + (places - fixed + offset_by * (used - fixed)) % max(1, amount - fixed)
        return jnp.zeros((amount,), jnp.int32).at[ranking[jnp.where(places < fixed, places, moved)]].set(jnp.asarray(sizes, jnp.int32))

    sizes = jnp.where(number % 4 == 0, named(heavy_load, number // 4), named(usual, number - number // 4 - 1))
    mixed = jax.random.permutation(jax.random.fold_in(own, 3), amount)
    donor, taker = mixed[0:amount // 2 * 2:2], mixed[1:amount // 2 * 2:2]
    room = jnp.minimum(sizes[donor] - 1, bound - sizes[taker]) // 2
    room = jnp.where((donor == ranking[0]) | (taker == ranking[0]) | (sizes[taker] == 0), 0, jnp.maximum(room, 0))
    moved = jax.random.randint(jax.random.fold_in(own, 4), (amount // 2,), 0, 1 << 20) % (room + 1)
    sizes = sizes.at[donor].add(-moved).at[taker].add(moved)
    labels = jnp.searchsorted(jnp.cumsum(sizes), jnp.arange(rows * top), side="right").astype(jnp.int32)
    listing = labels.reshape(top, rows).T
    listing = listing[jax.random.permutation(jax.random.fold_in(own, 1), rows)]
    offset_by = jax.random.randint(jax.random.fold_in(own, 2), (rows, 1), 0, top)
    return jnp.take_along_axis(listing, (jnp.arange(top)[None, :] + offset_by) % top, axis=1)


def load_shares(amount, total, most, skew, full):
    weights = [(1 << 20) // math.isqrt(standing ** skew) + 1 for standing in range(1, amount + 1)]
    largest = most if full else min(most, max(-(-total // amount), total * weights[0] // sum(weights)))
    least = 1 if total - largest >= amount - 1 else 0
    holding, rest = [largest] + [least] * (amount - 1), total - largest - least * (amount - 1)
    while rest > 0:
        free = [i for i in range(1, amount) if holding[i] < largest] or [i for i in range(1, amount) if holding[i] < most]
        pool, budget = sum([weights[i] for i in free]), rest
        for i in free:
            extra = min(most - holding[i], max(1, budget * weights[i] // pool), rest)
            holding[i] = holding[i] + extra
            rest = rest - extra
    return np.array(holding)


def gaussian(rng, shape, scale, reach, shards=(), dtype=jnp.bfloat16):
    values = jax.random.normal(rng, shape, jnp.float32) * scale
    if len(shards) > 0:
        values = block_levels(rng, shape, shards, -0.22, 0.18) * values
    return jnp.clip(values, min=-reach, max=reach).astype(dtype)


def setup_inputs(seed: int = 0, part: int = 0) -> dict:
    seeds = jax.random.split(jax.random.key(seed), 18)
    part_splits = jax.random.split(jax.random.fold_in(seeds[17], part), 18)
    ssm_input = gaussian(part_splits[0], (LEN, D_IN), 1.0, 6.0, ((0, 16),))
    gate_input = gaussian(part_splits[1], (LEN, D_IN), 1.0, 6.0, ((0, 16),))
    b_rows = gaussian(part_splits[2], (LEN, STATE), 1.0, 6.0, ((0, 16),))
    c_rows = gaussian(part_splits[3], (LEN, STATE), 1.0, 6.0, ((0, 16),))
    step_raw = draw_step_raw(jax.random.fold_in(jax.random.fold_in(seeds[17], part), 71), part)
    step_bias = jnp.clip(jax.random.uniform(seeds[5], (HEADS,), jnp.float32, -0.5, 0.5), -0.5, 0.5)
    rate_log = draw_rate_log(jax.random.fold_in(seeds[17], 71), part)
    skip_gain = jnp.clip(jax.random.uniform(seeds[7], (HEADS,), jnp.float32, 0.5, 2.0), 0.5, 2.0)
    norm_gain = jnp.clip(1.0 + 0.1 * jax.random.normal(seeds[8], (D_IN,), jnp.float32), 0.5, 1.5)
    w_out = gaussian(seeds[9], (D_IN, D), D_IN ** -0.5, 0.09375, ((1, 16),))
    residual = gaussian(part_splits[10], (LEN, D), 1.0, 6.0, ((0, 16),))
    moe_gain = jnp.clip(1.0 + 0.1 * jax.random.normal(seeds[11], (D,), jnp.float32), 0.5, 1.5)
    router = gaussian(seeds[12], (D, EXPERTS), D ** -0.5, 0.09375)
    expert_ids_keys = jax.random.split(jax.random.fold_in(part_splits[13], 1), LEN // TOK_DEV)
    expert_ids_turns = jax.random.permutation(jax.random.fold_in(part_splits[13], 3), LEN // TOK_DEV)
    expert_ids = jax.vmap(lambda own, number: shared_out(jax.random.fold_in(part_splits[13], 2), own, number, TOK_DEV, EXPERTS, TOP, CAP, 1))(expert_ids_keys, expert_ids_turns).reshape((LEN, TOP))
    w_gate = gaussian(seeds[14], (EXPERTS, D, FF), D ** -0.5, 0.09375, ((0, 16),))
    w_up = gaussian(seeds[15], (EXPERTS, D, FF), D ** -0.5, 0.09375, ((0, 16),))
    w_down = gaussian(seeds[16], (EXPERTS, FF, D), FF ** -0.5, 0.3125, ((0, 16),))
    return dict(ssm_input=ssm_input, gate_input=gate_input, b_rows=b_rows, c_rows=c_rows, step_raw=step_raw, step_bias=step_bias, rate_log=rate_log, skip_gain=skip_gain, norm_gain=norm_gain, w_out=w_out, residual=residual, moe_gain=moe_gain, router=router, expert_ids=expert_ids, w_gate=w_gate, w_up=w_up, w_down=w_down)


def group_pass(carried, pieces):
    inputs, b_block, c_block, steps_h, logs_h = pieces
    running = jnp.cumsum(logs_h, axis=0)
    length = logs_h.shape[0]
    scores = jnp.dot(c_block, b_block.T, preferred_element_type=jnp.float32)
    causal = jnp.arange(length)[:, None] >= jnp.arange(length)[None, :]
    spread = running[:, None, :] - running[None, :, :]
    decays = jnp.exp(jnp.where(causal[:, :, None], spread, -jnp.inf))
    mixing = (scores[:, :, None] * decays * steps_h[None, :, :]).astype(jnp.bfloat16)
    inputs32 = inputs.astype(jnp.float32)
    intra = jnp.einsum('tsh,shp->thp', mixing.astype(jnp.float32), inputs32, precision=lax.Precision.HIGHEST)
    c_wide = c_block.astype(jnp.float32)
    from_state = jnp.exp(running)[:, :, None] * jnp.einsum('tn,hpn->thp', c_wide, carried, precision=lax.Precision.HIGHEST)
    departing_state = jnp.exp(running[-1][None, :] - running) * steps_h
    block_in = (departing_state[:, :, None] * b_block.astype(jnp.float32)[:, None, :]).astype(jnp.bfloat16)
    update = jnp.einsum('shn,shp->hpn', block_in.astype(jnp.float32), inputs32, precision=lax.Precision.HIGHEST)
    new_carried = jnp.exp(running[-1])[:, None, None] * carried + update
    return (new_carried, intra + from_state)

def reference(ssm_input, gate_input, b_rows, c_rows, step_raw, step_bias, rate_log, skip_gain, norm_gain, w_out, residual, moe_gain, router, expert_ids, w_gate, w_up, w_down):
    blocks = LEN // GROUP
    step_sizes = jax.nn.softplus(step_raw + step_bias[None, :])
    log_decay = -step_sizes * jnp.exp(rate_log)[None, :]
    inputs = ssm_input.reshape(blocks, GROUP, HEADS, HEAD_DIM)
    pieces = (inputs, b_rows.reshape(blocks, GROUP, STATE), c_rows.reshape(blocks, GROUP, STATE), step_sizes.reshape(blocks, GROUP, HEADS), log_decay.reshape(blocks, GROUP, HEADS))
    start = jnp.zeros((HEADS, HEAD_DIM, STATE), jnp.float32)
    final_state, outputs = lax.scan(group_pass, start, pieces)
    ssm_out = outputs.reshape(LEN, HEADS, HEAD_DIM) + skip_gain[None, :, None] * ssm_input.reshape(LEN, HEADS, HEAD_DIM).astype(jnp.float32)
    gated = ssm_out.reshape(LEN, D_IN) * jax.nn.silu(gate_input.astype(jnp.float32))
    normed = (gated * lax.rsqrt(lax.optimization_barrier(jnp.mean(gated * gated, axis=1, keepdims=True)) + 1e-05) * norm_gain[None, :]).astype(jnp.bfloat16)
    mixer_out = jnp.dot(normed, w_out, preferred_element_type=jnp.float32).astype(jnp.bfloat16)
    hidden = (residual.astype(jnp.float32) + mixer_out.astype(jnp.float32)).astype(jnp.bfloat16)
    hidden_wide = hidden.astype(jnp.float32)
    moe_input = (hidden_wide * lax.rsqrt(lax.optimization_barrier(jnp.mean(hidden_wide * hidden_wide, axis=1, keepdims=True)) + 1e-05) * moe_gain[None, :]).astype(jnp.bfloat16)
    logits = jnp.dot(moe_input, router, preferred_element_type=jnp.float32)
    chosen = jnp.take_along_axis(logits, expert_ids, axis=1)
    powers = jnp.exp(chosen)
    combine = powers / lax.optimization_barrier(jnp.sum(powers, axis=1, keepdims=True))
    flat_ids = expert_ids.reshape(-1)
    flat_combine = combine.reshape(-1)
    capacity = N_SEQ * CAP
    total = hidden_wide
    for expert in range(EXPERTS):
        picked = flat_ids == expert
        count = jnp.sum(picked.astype(jnp.int32))
        rows = jnp.nonzero(picked, size=capacity, fill_value=0)[0].astype(jnp.int32)
        valid = (jnp.arange(capacity) < count).astype(jnp.float32)
        token_of = (rows // TOP).astype(jnp.int32)
        taken = moe_input[token_of]
        gate_part = jnp.dot(taken, w_gate[expert], preferred_element_type=jnp.float32)
        up_part = jnp.dot(taken, w_up[expert], preferred_element_type=jnp.float32)
        expert_hidden = (jax.nn.silu(gate_part) * up_part).astype(jnp.bfloat16)
        expert_out = jnp.dot(expert_hidden, w_down[expert], preferred_element_type=jnp.float32).astype(jnp.bfloat16)
        scaled = expert_out.astype(jnp.float32) * (flat_combine[rows] * valid)[:, None]
        total = total.at[token_of].add(scaled)
    return total.astype(jnp.bfloat16)
```

```python
import jax
import jax.numpy as jnp
from jax import lax
from jax.sharding import PartitionSpec as P

GROUP = 256


def group_pass(carried, pieces):
    inputs, b_block, c_block, steps_h, logs_h = pieces
    running = jnp.cumsum(logs_h, axis=0)
    length = logs_h.shape[0]
    scores = jnp.dot(c_block, b_block.T, preferred_element_type=jnp.float32)
    causal = jnp.arange(length)[:, None] >= jnp.arange(length)[None, :]
    spread = running[:, None, :] - running[None, :, :]
    decays = jnp.exp(jnp.where(causal[:, :, None], spread, -jnp.inf))
    mixing = (scores[:, :, None] * decays * steps_h[None, :, :]).astype(jnp.bfloat16)
    intra = jnp.einsum("tsh,shp->thp", mixing, inputs, preferred_element_type=jnp.float32)
    c_wide = c_block.astype(jnp.float32)
    from_state = jnp.exp(running)[:, :, None] * jnp.einsum(
        "tn,hpn->thp", c_wide, carried, precision=lax.Precision.HIGHEST
    )
    departing_state = jnp.exp(running[-1][None, :] - running) * steps_h
    block_in = (departing_state[:, :, None] * b_block.astype(jnp.float32)[:, None, :]).astype(
        jnp.bfloat16
    )
    update = jnp.einsum("shn,shp->hpn", block_in, inputs, preferred_element_type=jnp.float32)
    new_carried = jnp.exp(running[-1])[:, None, None] * carried + update
    return (new_carried, intra + from_state)


def shards(
    ssm_input,
    gate_input,
    b_rows,
    c_rows,
    step_raw,
    step_bias,
    rate_log,
    skip_gain,
    norm_gain,
    w_out,
    residual,
    moe_gain,
    router,
    expert_ids,
    w_gate,
    w_up,
    w_down,
):
    tokens_here = ssm_input.shape[0]
    inner = ssm_input.shape[1]
    heads = rate_log.shape[0]
    head_width = inner // heads
    state_width = b_rows.shape[1]
    blocks = tokens_here // GROUP
    step_sizes = jax.nn.softplus(step_raw + step_bias[None, :])
    log_decay = -step_sizes * jnp.exp(rate_log)[None, :]
    inputs = ssm_input.reshape(tokens_here, heads, head_width)
    pieces = (
        inputs.reshape(blocks, GROUP, heads, head_width),
        b_rows.reshape(blocks, GROUP, state_width),
        c_rows.reshape(blocks, GROUP, state_width),
        step_sizes.reshape(blocks, GROUP, heads),
        log_decay.reshape(blocks, GROUP, heads),
    )
    start = jnp.zeros((heads, head_width, state_width), jnp.float32)
    segment_state, outputs = lax.scan(group_pass, start, pieces)
    slab_log = jnp.cumsum(log_decay, axis=0)
    slab_total = slab_log[-1]
    n_seq = lax.axis_size("seq")
    per_chunk = heads // n_seq
    flat_state = segment_state.reshape(heads, head_width * state_width)
    packed = jnp.concatenate(
        [flat_state, jnp.broadcast_to(slab_total[:, None], (heads, 128))], axis=1
    ).reshape(n_seq, per_chunk, head_width * state_width + 128)
    received = lax.all_to_all(packed, "seq", 0, 0, tiled=True)
    slab_states = received[:, :, : head_width * state_width]
    slab_totals = received[:, :, head_width * state_width]

    def chain(entering_here, piece):
        state_j, total_j = piece
        return jnp.exp(total_j)[:, None] * entering_here + state_j, entering_here

    _, entering_each = lax.scan(
        chain, jnp.zeros((per_chunk, head_width * state_width), jnp.float32), (slab_states, slab_totals)
    )
    entering = lax.all_to_all(entering_each, "seq", 0, 0, tiled=True).reshape(
        heads, head_width, state_width
    )
    c_wide = c_rows.astype(jnp.float32)
    arriving = jnp.exp(slab_log)[:, :, None] * jnp.einsum(
        "tn,hpn->thp", c_wide, entering, precision=lax.Precision.HIGHEST
    )
    ssm_out = (
        outputs.reshape(tokens_here, heads, head_width)
        + arriving
        + skip_gain[None, :, None] * inputs.astype(jnp.float32)
    )
    gated = ssm_out.reshape(tokens_here, inner) * jax.nn.silu(gate_input.astype(jnp.float32))
    normed = (
        gated
        * lax.rsqrt(jnp.mean(gated * gated, axis=1, keepdims=True) + 1e-05)
        * norm_gain[None, :]
    ).astype(jnp.bfloat16)
    w_full = lax.all_gather(w_out, "seq", axis=1, tiled=True)
    mixer_out = jnp.dot(normed, w_full, preferred_element_type=jnp.float32).astype(jnp.bfloat16)
    hidden = (residual.astype(jnp.float32) + mixer_out.astype(jnp.float32)).astype(jnp.bfloat16)
    hidden_wide = hidden.astype(jnp.float32)
    moe_input = (
        hidden_wide
        * lax.rsqrt(jnp.mean(hidden_wide * hidden_wide, axis=1, keepdims=True) + 1e-05)
        * moe_gain[None, :]
    ).astype(jnp.bfloat16)
    logits = jnp.dot(moe_input, router, preferred_element_type=jnp.float32)
    chosen = jnp.take_along_axis(logits, expert_ids, axis=1)
    powers = jnp.exp(chosen)
    combine = powers / jnp.sum(powers, axis=1, keepdims=True)
    experts_all = lax.axis_size("seq")
    fanout = expert_ids.shape[1]
    capacity = tokens_here * fanout * 3 // (2 * experts_all)
    width = moe_input.shape[1]
    flat_ids = expert_ids.reshape(-1)
    one_hot = (flat_ids[:, None] == jnp.arange(experts_all, dtype=jnp.int32)[None, :]).astype(
        jnp.int32
    )
    running_count = jnp.cumsum(one_hot, axis=0)
    slot_of = jnp.sum(running_count * one_hot, axis=1) - 1
    target = flat_ids * capacity + slot_of
    repeated = jnp.repeat(moe_input, fanout, axis=0)
    departing_state = (
        jnp.zeros((experts_all * capacity, width), jnp.bfloat16).at[target].set(repeated)
    )
    departing_state = departing_state.reshape(experts_all, capacity, width)
    batch = lax.all_to_all(departing_state, "seq", split_axis=0, concat_axis=0, tiled=True)
    flat_rows = batch.reshape(-1, width)
    gate_part = jnp.dot(flat_rows, w_gate[0], preferred_element_type=jnp.float32)
    up_part = jnp.dot(flat_rows, w_up[0], preferred_element_type=jnp.float32)
    expert_hidden = (jax.nn.silu(gate_part) * up_part).astype(jnp.bfloat16)
    result = jnp.dot(expert_hidden, w_down[0], preferred_element_type=jnp.float32).astype(
        jnp.bfloat16
    )
    finished = result.reshape(batch.shape)
    returned = lax.all_to_all(finished, "seq", split_axis=0, concat_axis=0, tiled=True).reshape(
        experts_all * capacity, width
    )
    fetched = returned[target].astype(jnp.float32).reshape(tokens_here, fanout, width)
    total = hidden_wide + jnp.sum(combine[:, :, None] * fetched, axis=1)
    return total.astype(jnp.bfloat16)


def solution(mesh):
    in_specs = (
        P(("batch", "seq"), None),
        P(("batch", "seq"), None),
        P(("batch", "seq"), None),
        P(("batch", "seq"), None),
        P(("batch", "seq"), None),
        P(),
        P(),
        P(),
        P(),
        P(None, "seq"),
        P(("batch", "seq"), None),
        P(),
        P(),
        P(("batch", "seq"), None),
        P("seq", None, None),
        P("seq", None, None),
        P("seq", None, None),
    )
    out_specs = P(("batch", "seq"), None)
    return jax.shard_map(shards, mesh=mesh, in_specs=in_specs, out_specs=out_specs, check_vma=False)
```

```python
import jax
import jax.numpy as jnp
from jax import lax
from jax.sharding import PartitionSpec as P

GROUP = 256


def group_pass(carried, pieces):
    inputs, b_block, c_block, steps_h, logs_h = pieces
    running = jnp.cumsum(logs_h, axis=0)
    length = logs_h.shape[0]
    scores = jnp.dot(c_block, b_block.T, preferred_element_type=jnp.float32)
    causal = jnp.arange(length)[:, None] >= jnp.arange(length)[None, :]
    spread = running[:, None, :] - running[None, :, :]
    decays = jnp.exp(jnp.where(causal[:, :, None], spread, -jnp.inf))
    mixing = (scores[:, :, None] * decays * steps_h[None, :, :]).astype(jnp.bfloat16)
    intra = jnp.einsum("tsh,shp->thp", mixing, inputs, preferred_element_type=jnp.float32)
    c_wide = c_block.astype(jnp.float32)
    from_state = jnp.exp(running)[:, :, None] * jnp.einsum(
        "tn,hpn->thp", c_wide, carried, precision=lax.Precision.HIGHEST
    )
    departing_state = jnp.exp(running[-1][None, :] - running) * steps_h
    block_in = (departing_state[:, :, None] * b_block.astype(jnp.float32)[:, None, :]).astype(
        jnp.bfloat16
    )
    update = jnp.einsum("shn,shp->hpn", block_in, inputs, preferred_element_type=jnp.float32)
    new_carried = jnp.exp(running[-1])[:, None, None] * carried + update
    return (new_carried, intra + from_state)


def shards(
    ssm_input,
    gate_input,
    b_rows,
    c_rows,
    step_raw,
    step_bias,
    rate_log,
    skip_gain,
    norm_gain,
    w_out,
    residual,
    moe_gain,
    router,
    expert_ids,
    w_gate,
    w_up,
    w_down,
):
    tokens_here = ssm_input.shape[0]
    inner = ssm_input.shape[1]
    heads = rate_log.shape[0]
    head_width = inner // heads
    state_width = b_rows.shape[1]
    blocks = tokens_here // GROUP
    step_sizes = jax.nn.softplus(step_raw + step_bias[None, :])
    log_decay = -step_sizes * jnp.exp(rate_log)[None, :]
    inputs = ssm_input.reshape(tokens_here, heads, head_width)
    pieces = (
        inputs.reshape(blocks, GROUP, heads, head_width),
        b_rows.reshape(blocks, GROUP, state_width),
        c_rows.reshape(blocks, GROUP, state_width),
        step_sizes.reshape(blocks, GROUP, heads),
        log_decay.reshape(blocks, GROUP, heads),
    )
    start = jnp.zeros((heads, head_width, state_width), jnp.float32)
    segment_state, outputs = lax.scan(group_pass, start, pieces)
    slab_log = jnp.cumsum(log_decay, axis=0)
    slab_total = slab_log[-1]
    n_seq = lax.axis_size("seq")
    per_chunk = heads // n_seq
    flat_state = segment_state.reshape(heads, head_width * state_width)
    packed = jnp.concatenate(
        [flat_state, jnp.broadcast_to(slab_total[:, None], (heads, 128))], axis=1
    ).reshape(n_seq, per_chunk, head_width * state_width + 128)
    received = lax.all_to_all(packed, "seq", 0, 0, tiled=True)
    slab_states = received[:, :, : head_width * state_width]
    slab_totals = received[:, :, head_width * state_width]

    entering_here = jnp.zeros((per_chunk, head_width * state_width), jnp.float32)
    entering_list = []
    for j in range(n_seq):
        entering_list.append(entering_here)
        entering_here = jnp.exp(slab_totals[j])[:, None] * entering_here + slab_states[j]
    entering_each = jnp.stack(entering_list)
    entering = lax.all_to_all(entering_each, "seq", 0, 0, tiled=True).reshape(
        heads, head_width, state_width
    )
    c_wide = c_rows.astype(jnp.float32)
    arriving = jnp.exp(slab_log)[:, :, None] * jnp.einsum(
        "tn,hpn->thp", c_wide, entering, precision=lax.Precision.HIGHEST
    )
    ssm_out = (
        outputs.reshape(tokens_here, heads, head_width)
        + arriving
        + skip_gain[None, :, None] * inputs.astype(jnp.float32)
    )
    gated = ssm_out.reshape(tokens_here, inner) * jax.nn.silu(gate_input.astype(jnp.float32))
    normed = (
        gated
        * lax.rsqrt(jnp.mean(gated * gated, axis=1, keepdims=True) + 1e-05)
        * norm_gain[None, :]
    ).astype(jnp.bfloat16)
    n_batch = lax.axis_size("batch")
    core = lax.axis_index("batch") % 2
    shard_cols = w_out.shape[1]
    half = shard_cols // 2
    w_half = lax.all_gather(
        lax.dynamic_slice_in_dim(w_out, core * half, half, axis=1), "seq", axis=1, tiled=True
    )
    partners = [(b, b ^ 1) for b in range(n_batch)]
    normed_partner = lax.ppermute(normed, "batch", partners)
    own_half = jnp.dot(normed, w_half, preferred_element_type=jnp.float32).astype(jnp.bfloat16)
    partner_half = jnp.dot(normed_partner, w_half, preferred_element_type=jnp.float32).astype(
        jnp.bfloat16
    )
    other_half = lax.ppermute(partner_half, "batch", partners)
    first_half = jnp.where(core == 0, own_half, other_half)
    second_half = jnp.where(core == 0, other_half, own_half)
    mixer_out = jnp.stack(
        [
            first_half.reshape(tokens_here, n_seq, half),
            second_half.reshape(tokens_here, n_seq, half),
        ],
        axis=2,
    ).reshape(tokens_here, n_seq * shard_cols)
    hidden = (residual.astype(jnp.float32) + mixer_out.astype(jnp.float32)).astype(jnp.bfloat16)
    hidden_wide = hidden.astype(jnp.float32)
    moe_input = (
        hidden_wide
        * lax.rsqrt(jnp.mean(hidden_wide * hidden_wide, axis=1, keepdims=True) + 1e-05)
        * moe_gain[None, :]
    ).astype(jnp.bfloat16)
    logits = jnp.dot(moe_input, router, preferred_element_type=jnp.float32)
    chosen = jnp.take_along_axis(logits, expert_ids, axis=1)
    powers = jnp.exp(chosen)
    combine = powers / jnp.sum(powers, axis=1, keepdims=True)
    experts_all = lax.axis_size("seq")
    fanout = expert_ids.shape[1]
    capacity = tokens_here * fanout * 3 // (2 * experts_all)
    width = moe_input.shape[1]
    flat_ids = expert_ids.reshape(-1)
    one_hot = (flat_ids[:, None] == jnp.arange(experts_all, dtype=jnp.int32)[None, :]).astype(
        jnp.int32
    )
    running_count = jnp.cumsum(one_hot, axis=0)
    slot_of = jnp.sum(running_count * one_hot, axis=1) - 1
    target = flat_ids * capacity + slot_of
    slots = experts_all * capacity
    target_pairs = target.reshape(tokens_here, fanout)
    slot_ids = jnp.arange(slots, dtype=jnp.int32)
    placing = jnp.zeros((slots, tokens_here), jnp.bool_)
    for k in range(fanout):
        placing = placing | (slot_ids[:, None] == target_pairs[None, :, k])
    departing_state = jnp.dot(
        placing.astype(jnp.bfloat16), moe_input, preferred_element_type=jnp.float32
    ).astype(jnp.bfloat16)
    departing_state = departing_state.reshape(experts_all, capacity, width)
    batch = lax.all_to_all(departing_state, "seq", split_axis=0, concat_axis=0, tiled=True)
    flat_rows = batch.reshape(-1, width)
    gate_part = jnp.dot(flat_rows, w_gate[0], preferred_element_type=jnp.float32)
    up_part = jnp.dot(flat_rows, w_up[0], preferred_element_type=jnp.float32)
    expert_hidden = (jax.nn.silu(gate_part) * up_part).astype(jnp.bfloat16)
    result = jnp.dot(expert_hidden, w_down[0], preferred_element_type=jnp.float32).astype(
        jnp.bfloat16
    )
    finished = result.reshape(batch.shape)
    returned = lax.all_to_all(finished, "seq", split_axis=0, concat_axis=0, tiled=True).reshape(
        experts_all * capacity, width
    )
    total = hidden_wide
    for k in range(fanout):
        picking = (target_pairs[:, k][:, None] == slot_ids[None, :]).astype(jnp.bfloat16)
        fetched = jnp.dot(picking, returned, preferred_element_type=jnp.float32)
        total = total + combine[:, k][:, None] * fetched
    return total.astype(jnp.bfloat16)


def solution(mesh):
    in_specs = (
        P(("batch", "seq"), None),
        P(("batch", "seq"), None),
        P(("batch", "seq"), None),
        P(("batch", "seq"), None),
        P(("batch", "seq"), None),
        P(),
        P(),
        P(),
        P(),
        P(None, "seq"),
        P(("batch", "seq"), None),
        P(),
        P(),
        P(("batch", "seq"), None),
        P("seq", None, None),
        P("seq", None, None),
        P("seq", None, None),
    )
    out_specs = P(("batch", "seq"), None)
    return jax.shard_map(shards, mesh=mesh, in_specs=in_specs, out_specs=out_specs, check_vma=False)
```

```python
import jax
import jax.numpy as jnp
from jax import lax
from jax.sharding import PartitionSpec as P

GROUP = 256


def group_pass(carried, pieces):
    inputs, b_block, c_block, steps_h, logs_h = pieces
    running = jnp.cumsum(logs_h, axis=0)
    length = logs_h.shape[0]
    scores = jnp.dot(c_block, b_block.T, preferred_element_type=jnp.float32)
    causal = jnp.arange(length)[:, None] >= jnp.arange(length)[None, :]
    spread = running[:, None, :] - running[None, :, :]
    decays = jnp.exp(jnp.where(causal[:, :, None], spread, -jnp.inf))
    mixing = (scores[:, :, None] * decays * steps_h[None, :, :]).astype(jnp.bfloat16)
    intra = jnp.einsum("tsh,shp->thp", mixing, inputs, preferred_element_type=jnp.float32)
    c_wide = c_block.astype(jnp.float32)
    from_state = jnp.exp(running)[:, :, None] * jnp.einsum(
        "tn,hpn->thp", c_wide, carried, precision=lax.Precision.HIGHEST
    )
    departing_state = jnp.exp(running[-1][None, :] - running) * steps_h
    block_in = (departing_state[:, :, None] * b_block.astype(jnp.float32)[:, None, :]).astype(
        jnp.bfloat16
    )
    update = jnp.einsum("shn,shp->hpn", block_in, inputs, preferred_element_type=jnp.float32)
    new_carried = jnp.exp(running[-1])[:, None, None] * carried + update
    return (new_carried, intra + from_state)


def shards(
    ssm_input,
    gate_input,
    b_rows,
    c_rows,
    step_raw,
    step_bias,
    rate_log,
    skip_gain,
    norm_gain,
    w_out,
    residual,
    moe_gain,
    router,
    expert_ids,
    w_gate,
    w_up,
    w_down,
):
    tokens_here = ssm_input.shape[0]
    inner = ssm_input.shape[1]
    heads = rate_log.shape[0]
    head_width = inner // heads
    state_width = b_rows.shape[1]
    blocks = tokens_here // GROUP
    step_sizes = jax.nn.softplus(step_raw + step_bias[None, :])
    log_decay = -step_sizes * jnp.exp(rate_log)[None, :]
    inputs = ssm_input.reshape(tokens_here, heads, head_width)
    pieces = (
        inputs.reshape(blocks, GROUP, heads, head_width),
        b_rows.reshape(blocks, GROUP, state_width),
        c_rows.reshape(blocks, GROUP, state_width),
        step_sizes.reshape(blocks, GROUP, heads),
        log_decay.reshape(blocks, GROUP, heads),
    )
    start = jnp.zeros((heads, head_width, state_width), jnp.float32)
    segment_state, outputs = lax.scan(group_pass, start, pieces)
    slab_log = jnp.cumsum(log_decay, axis=0)
    slab_total = slab_log[-1]
    n_seq = lax.axis_size("seq")
    per_chunk = heads // n_seq
    flat_state = segment_state.reshape(heads, head_width * state_width)
    with jax.named_scope("state_pack"):
        packed = jnp.concatenate(
            [flat_state, jnp.broadcast_to(slab_total[:, None], (heads, 128))], axis=1
        ).reshape(n_seq, per_chunk, head_width * state_width + 128)
    received = lax.all_to_all(packed, "seq", 0, 0, tiled=True)
    slab_states = received[:, :, : head_width * state_width]
    slab_totals = received[:, :, head_width * state_width]

    order = jnp.arange(n_seq)
    between = (order[None, None, :] > order[None, :, None]) & (order[None, None, :] < order[:, None, None])
    span = jnp.sum(jnp.where(between[:, :, :, None], slab_totals[None, None, :, :], 0.0), axis=2)
    earlier = (order[:, None] > order[None, :])[:, :, None]
    carry_weights = jnp.where(earlier, jnp.exp(span), 0.0)
    entering_each = jnp.einsum(
        "ijh,jhx->ihx", carry_weights, slab_states, precision=lax.Precision.HIGHEST
    )
    entering = lax.all_to_all(entering_each, "seq", 0, 0, tiled=True).reshape(
        heads, head_width, state_width
    )
    c_wide = c_rows.astype(jnp.float32)
    arriving = jnp.exp(slab_log)[:, :, None] * jnp.einsum(
        "tn,hpn->thp", c_wide, entering, precision=lax.Precision.HIGHEST
    )
    ssm_out = (
        outputs.reshape(tokens_here, heads, head_width)
        + arriving
        + skip_gain[None, :, None] * inputs.astype(jnp.float32)
    )
    gated = ssm_out.reshape(tokens_here, inner) * jax.nn.silu(gate_input.astype(jnp.float32))
    normed = (
        gated
        * lax.rsqrt(jnp.mean(gated * gated, axis=1, keepdims=True) + 1e-05)
        * norm_gain[None, :]
    ).astype(jnp.bfloat16)
    n_batch = lax.axis_size("batch")
    core = lax.axis_index("batch") % 2
    depth = w_out.shape[0] // 2
    with jax.named_scope("wgather"):
        w_rows = lax.all_gather(
            lax.dynamic_slice_in_dim(w_out, core * depth, depth, axis=0), "seq", axis=1, tiled=True
        )
    partners = [(b, b ^ 1) for b in range(n_batch)]
    own_rows = lax.dynamic_slice_in_dim(normed, core * depth, depth, axis=1)
    partner_rows = lax.ppermute(
        lax.dynamic_slice_in_dim(normed, (1 - core) * depth, depth, axis=1), "batch", partners
    )
    own_part = jnp.dot(own_rows, w_rows, preferred_element_type=jnp.float32)
    partner_part = jnp.dot(partner_rows, w_rows, preferred_element_type=jnp.float32)
    other_part = lax.ppermute(partner_part, "batch", partners)
    mixer_out = (own_part + other_part).astype(jnp.bfloat16)
    hidden = (residual.astype(jnp.float32) + mixer_out.astype(jnp.float32)).astype(jnp.bfloat16)
    hidden_wide = hidden.astype(jnp.float32)
    moe_input = (
        hidden_wide
        * lax.rsqrt(jnp.mean(hidden_wide * hidden_wide, axis=1, keepdims=True) + 1e-05)
        * moe_gain[None, :]
    ).astype(jnp.bfloat16)
    logits = jnp.dot(moe_input, router, preferred_element_type=jnp.float32)
    chosen = jnp.take_along_axis(logits, expert_ids, axis=1)
    powers = jnp.exp(chosen)
    combine = powers / jnp.sum(powers, axis=1, keepdims=True)
    experts_all = lax.axis_size("seq")
    fanout = expert_ids.shape[1]
    capacity = tokens_here * fanout * 3 // (2 * experts_all)
    width = moe_input.shape[1]
    flat_ids = expert_ids.reshape(-1)
    one_hot = (flat_ids[:, None] == jnp.arange(experts_all, dtype=jnp.int32)[None, :]).astype(
        jnp.int32
    )
    running_count = jnp.cumsum(one_hot, axis=0)
    slot_of = jnp.sum(running_count * one_hot, axis=1) - 1
    target = flat_ids * capacity + slot_of
    slots = experts_all * capacity
    target_pairs = target.reshape(tokens_here, fanout)
    slot_ids = jnp.arange(slots, dtype=jnp.int32)
    placing = jnp.zeros((slots, tokens_here), jnp.bool_)
    for k in range(fanout):
        placing = placing | (slot_ids[:, None] == target_pairs[None, :, k])
    departing_state = jnp.dot(
        placing.astype(jnp.bfloat16), moe_input, preferred_element_type=jnp.float32
    ).astype(jnp.bfloat16)
    departing_state = departing_state.reshape(experts_all, capacity, width)
    batch = lax.all_to_all(departing_state, "seq", split_axis=0, concat_axis=0, tiled=True)
    flat_rows = batch.reshape(-1, width)
    gate_part = jnp.dot(flat_rows, w_gate[0], preferred_element_type=jnp.float32)
    up_part = jnp.dot(flat_rows, w_up[0], preferred_element_type=jnp.float32)
    expert_hidden = (jax.nn.silu(gate_part) * up_part).astype(jnp.bfloat16)
    result = jnp.dot(expert_hidden, w_down[0], preferred_element_type=jnp.float32).astype(
        jnp.bfloat16
    )
    finished = result.reshape(batch.shape)
    returned = lax.all_to_all(finished, "seq", split_axis=0, concat_axis=0, tiled=True).reshape(
        experts_all * capacity, width
    )
    total = hidden_wide
    for k in range(fanout):
        picking = (target_pairs[:, k][:, None] == slot_ids[None, :]).astype(jnp.bfloat16)
        fetched = jnp.dot(picking, returned, preferred_element_type=jnp.float32)
        total = total + combine[:, k][:, None] * fetched
    return total.astype(jnp.bfloat16)


def solution(mesh):
    in_specs = (
        P(("batch", "seq"), None),
        P(("batch", "seq"), None),
        P(("batch", "seq"), None),
        P(("batch", "seq"), None),
        P(("batch", "seq"), None),
        P(),
        P(),
        P(),
        P(),
        P(None, "seq"),
        P(("batch", "seq"), None),
        P(),
        P(),
        P(("batch", "seq"), None),
        P("seq", None, None),
        P("seq", None, None),
        P("seq", None, None),
    )
    out_specs = P(("batch", "seq"), None)
    return jax.shard_map(shards, mesh=mesh, in_specs=in_specs, out_specs=out_specs, check_vma=False)
```

```python
import jax
import jax.numpy as jnp
from jax import lax
from jax.sharding import PartitionSpec as P

GROUP = 256


def group_pass(carried, pieces):
    inputs, b_block, c_block, steps_h, logs_h = pieces
    running = jnp.cumsum(logs_h, axis=0)
    length = logs_h.shape[0]
    scores = jnp.dot(c_block, b_block.T, preferred_element_type=jnp.float32)
    causal = jnp.arange(length)[:, None] >= jnp.arange(length)[None, :]
    spread = running[:, None, :] - running[None, :, :]
    decays = jnp.exp(jnp.where(causal[:, :, None], spread, -jnp.inf))
    mixing = (scores[:, :, None] * decays * steps_h[None, :, :]).astype(jnp.bfloat16)
    intra = jnp.einsum("tsh,shp->thp", mixing, inputs, preferred_element_type=jnp.float32)
    c_wide = c_block.astype(jnp.float32)
    from_state = jnp.exp(running)[:, :, None] * jnp.einsum(
        "tn,hpn->thp", c_wide, carried, precision=lax.Precision.HIGHEST
    )
    departing_state = jnp.exp(running[-1][None, :] - running) * steps_h
    block_in = (departing_state[:, :, None] * b_block.astype(jnp.float32)[:, None, :]).astype(
        jnp.bfloat16
    )
    update = jnp.einsum("shn,shp->hpn", block_in, inputs, preferred_element_type=jnp.float32)
    new_carried = jnp.exp(running[-1])[:, None, None] * carried + update
    return (new_carried, intra + from_state)


def shards(
    ssm_input,
    gate_input,
    b_rows,
    c_rows,
    step_raw,
    step_bias,
    rate_log,
    skip_gain,
    norm_gain,
    w_out,
    residual,
    moe_gain,
    router,
    expert_ids,
    w_gate,
    w_up,
    w_down,
):
    tokens_here = ssm_input.shape[0]
    inner = ssm_input.shape[1]
    heads = rate_log.shape[0]
    head_width = inner // heads
    state_width = b_rows.shape[1]
    blocks = tokens_here // GROUP
    step_sizes = jax.nn.softplus(step_raw + step_bias[None, :])
    log_decay = -step_sizes * jnp.exp(rate_log)[None, :]
    inputs = ssm_input.reshape(tokens_here, heads, head_width)
    pieces = (
        inputs.reshape(blocks, GROUP, heads, head_width),
        b_rows.reshape(blocks, GROUP, state_width),
        c_rows.reshape(blocks, GROUP, state_width),
        step_sizes.reshape(blocks, GROUP, heads),
        log_decay.reshape(blocks, GROUP, heads),
    )
    start = jnp.zeros((heads, head_width, state_width), jnp.float32)
    segment_state, outputs = lax.scan(group_pass, start, pieces)
    slab_log = jnp.cumsum(log_decay, axis=0)
    slab_total = slab_log[-1]
    n_seq = lax.axis_size("seq")
    per_chunk = heads // n_seq
    flat_state = segment_state.reshape(heads, head_width * state_width)
    with jax.named_scope("state_pack"):
        packed = jnp.concatenate(
            [flat_state, jnp.broadcast_to(slab_total[:, None], (heads, 128))], axis=1
        ).reshape(n_seq, per_chunk, head_width * state_width + 128)
    received = lax.all_to_all(packed, "seq", 0, 0, tiled=True)
    slab_states = received[:, :, : head_width * state_width]
    slab_totals = received[:, :, head_width * state_width]

    order = jnp.arange(n_seq)
    between = (order[None, None, :] > order[None, :, None]) & (order[None, None, :] < order[:, None, None])
    span = jnp.sum(jnp.where(between[:, :, :, None], slab_totals[None, None, :, :], 0.0), axis=2)
    earlier = (order[:, None] > order[None, :])[:, :, None]
    carry_weights = jnp.where(earlier, jnp.exp(span), 0.0)
    entering_each = jnp.einsum(
        "ijh,jhx->ihx", carry_weights, slab_states, precision=lax.Precision.HIGHEST
    )
    entering = lax.all_to_all(entering_each, "seq", 0, 0, tiled=True).reshape(
        heads, head_width, state_width
    )
    c_wide = c_rows.astype(jnp.float32)
    arriving = jnp.exp(slab_log)[:, :, None] * jnp.einsum(
        "tn,hpn->thp", c_wide, entering, precision=lax.Precision.HIGHEST
    )
    ssm_out = (
        outputs.reshape(tokens_here, heads, head_width)
        + arriving
        + skip_gain[None, :, None] * inputs.astype(jnp.float32)
    )
    gated = ssm_out.reshape(tokens_here, inner) * jax.nn.silu(gate_input.astype(jnp.float32))
    normed = (
        gated
        * lax.rsqrt(jnp.mean(gated * gated, axis=1, keepdims=True) + 1e-05)
        * norm_gain[None, :]
    ).astype(jnp.bfloat16)
    n_batch = lax.axis_size("batch")
    core = lax.axis_index("batch") % 2
    depth = w_out.shape[0] // 2
    with jax.named_scope("wgather"):
        w_rows = lax.all_gather(
            lax.dynamic_slice_in_dim(w_out, core * depth, depth, axis=0), "seq", axis=1, tiled=True
        )
    partners = [(b, b ^ 1) for b in range(n_batch)]
    own_rows = lax.dynamic_slice_in_dim(normed, core * depth, depth, axis=1)
    partner_rows = lax.ppermute(
        lax.dynamic_slice_in_dim(normed, (1 - core) * depth, depth, axis=1), "batch", partners
    )
    both_parts = jnp.dot(
        jnp.concatenate([partner_rows, own_rows], axis=0), w_rows, preferred_element_type=jnp.float32
    )
    partner_part = both_parts[:tokens_here]
    own_part = both_parts[tokens_here:]
    other_part = lax.ppermute(partner_part, "batch", partners)
    mixer_out = (own_part + other_part).astype(jnp.bfloat16)
    hidden = (residual.astype(jnp.float32) + mixer_out.astype(jnp.float32)).astype(jnp.bfloat16)
    hidden_wide = hidden.astype(jnp.float32)
    moe_input = (
        hidden_wide
        * lax.rsqrt(jnp.mean(hidden_wide * hidden_wide, axis=1, keepdims=True) + 1e-05)
        * moe_gain[None, :]
    ).astype(jnp.bfloat16)
    logits = jnp.dot(moe_input, router, preferred_element_type=jnp.float32)
    chosen = jnp.take_along_axis(logits, expert_ids, axis=1)
    powers = jnp.exp(chosen)
    combine = powers / jnp.sum(powers, axis=1, keepdims=True)
    experts_all = lax.axis_size("seq")
    fanout = expert_ids.shape[1]
    capacity = tokens_here * fanout * 3 // (2 * experts_all)
    width = moe_input.shape[1]
    flat_ids = expert_ids.reshape(-1)
    one_hot = (flat_ids[:, None] == jnp.arange(experts_all, dtype=jnp.int32)[None, :]).astype(
        jnp.int32
    )
    running_count = jnp.cumsum(one_hot, axis=0)
    slot_of = jnp.sum(running_count * one_hot, axis=1) - 1
    target = flat_ids * capacity + slot_of
    slots = experts_all * capacity
    target_pairs = target.reshape(tokens_here, fanout)
    stages = 2
    chunk = capacity // stages
    slot_grid = jnp.arange(slots, dtype=jnp.int32).reshape(experts_all, stages, chunk)
    total = hidden_wide
    for h in range(stages):
        slot_ids = slot_grid[:, h, :].reshape(-1)
        placing = jnp.zeros((slot_ids.shape[0], tokens_here), jnp.bool_)
        for k in range(fanout):
            placing = placing | (slot_ids[:, None] == target_pairs[None, :, k])
        departing_state = jnp.dot(
            placing.astype(jnp.bfloat16), moe_input, preferred_element_type=jnp.float32
        ).astype(jnp.bfloat16)
        departing_state = departing_state.reshape(experts_all, chunk, width)
        batch = lax.all_to_all(departing_state, "seq", split_axis=0, concat_axis=0, tiled=True)
        flat_rows = batch.reshape(-1, width)
        gate_part = jnp.dot(flat_rows, w_gate[0], preferred_element_type=jnp.float32)
        up_part = jnp.dot(flat_rows, w_up[0], preferred_element_type=jnp.float32)
        expert_hidden = (jax.nn.silu(gate_part) * up_part).astype(jnp.bfloat16)
        result = jnp.dot(expert_hidden, w_down[0], preferred_element_type=jnp.float32).astype(
            jnp.bfloat16
        )
        finished = result.reshape(batch.shape)
        returned = lax.all_to_all(
            finished, "seq", split_axis=0, concat_axis=0, tiled=True
        ).reshape(-1, width)
        for k in range(fanout):
            picking = (target_pairs[:, k][:, None] == slot_ids[None, :]).astype(jnp.bfloat16)
            fetched = jnp.dot(picking, returned, preferred_element_type=jnp.float32)
            total = total + combine[:, k][:, None] * fetched
    return total.astype(jnp.bfloat16)


def solution(mesh):
    in_specs = (
        P(("batch", "seq"), None),
        P(("batch", "seq"), None),
        P(("batch", "seq"), None),
        P(("batch", "seq"), None),
        P(("batch", "seq"), None),
        P(),
        P(),
        P(),
        P(),
        P(None, "seq"),
        P(("batch", "seq"), None),
        P(),
        P(),
        P(("batch", "seq"), None),
        P("seq", None, None),
        P("seq", None, None),
        P("seq", None, None),
    )
    out_specs = P(("batch", "seq"), None)
    return jax.shard_map(shards, mesh=mesh, in_specs=in_specs, out_specs=out_specs, check_vma=False)
```

```python
import jax
import jax.numpy as jnp
from jax import lax
from jax.sharding import PartitionSpec as P

GROUP = 256


def group_pass(carried, pieces):
    inputs, b_block, c_block, steps_h, logs_h = pieces
    running = jnp.cumsum(logs_h, axis=0)
    length = logs_h.shape[0]
    scores = jnp.dot(c_block, b_block.T, preferred_element_type=jnp.float32)
    causal = jnp.arange(length)[:, None] >= jnp.arange(length)[None, :]
    spread = running[:, None, :] - running[None, :, :]
    decays = jnp.exp(jnp.where(causal[:, :, None], spread, -jnp.inf))
    mixing = (scores[:, :, None] * decays * steps_h[None, :, :]).astype(jnp.bfloat16)
    intra = jnp.einsum("tsh,shp->thp", mixing, inputs, preferred_element_type=jnp.float32)
    c_wide = c_block.astype(jnp.float32)
    from_state = jnp.exp(running)[:, :, None] * jnp.einsum(
        "tn,hpn->thp", c_wide, carried, precision=lax.Precision.HIGHEST
    )
    departing_state = jnp.exp(running[-1][None, :] - running) * steps_h
    block_in = (departing_state[:, :, None] * b_block.astype(jnp.float32)[:, None, :]).astype(
        jnp.bfloat16
    )
    update = jnp.einsum("shn,shp->hpn", block_in, inputs, preferred_element_type=jnp.float32)
    new_carried = jnp.exp(running[-1])[:, None, None] * carried + update
    return (new_carried, intra + from_state)


def shards(
    ssm_input,
    gate_input,
    b_rows,
    c_rows,
    step_raw,
    step_bias,
    rate_log,
    skip_gain,
    norm_gain,
    w_out,
    residual,
    moe_gain,
    router,
    expert_ids,
    w_gate,
    w_up,
    w_down,
):
    tokens_here = ssm_input.shape[0]
    inner = ssm_input.shape[1]
    heads = rate_log.shape[0]
    head_width = inner // heads
    state_width = b_rows.shape[1]
    blocks = tokens_here // GROUP
    step_sizes = jax.nn.softplus(step_raw + step_bias[None, :])
    log_decay = -step_sizes * jnp.exp(rate_log)[None, :]
    inputs = ssm_input.reshape(tokens_here, heads, head_width)
    pieces = (
        inputs.reshape(blocks, GROUP, heads, head_width),
        b_rows.reshape(blocks, GROUP, state_width),
        c_rows.reshape(blocks, GROUP, state_width),
        step_sizes.reshape(blocks, GROUP, heads),
        log_decay.reshape(blocks, GROUP, heads),
    )
    start = jnp.zeros((heads, head_width, state_width), jnp.float32)
    segment_state, outputs = lax.scan(group_pass, start, pieces)
    slab_log = jnp.cumsum(log_decay, axis=0)
    slab_total = slab_log[-1]
    n_seq = lax.axis_size("seq")
    per_chunk = heads // n_seq
    chunk_rows = per_chunk * head_width
    state_rows = segment_state.reshape(n_seq, chunk_rows, state_width)
    total_rows = jnp.broadcast_to(slab_total.reshape(n_seq, per_chunk, 1), (n_seq, per_chunk, state_width))
    total_block = jnp.pad(total_rows, ((0, 0), (0, 8 - per_chunk), (0, 0)))
    packed = jnp.concatenate([state_rows, total_block], axis=1)
    received = lax.all_to_all(packed, "seq", 0, 0, tiled=True)
    slab_states = received[:, :chunk_rows].reshape(n_seq, per_chunk, head_width, state_width)
    slab_totals = received[:, chunk_rows : chunk_rows + per_chunk, 0]
    order = jnp.arange(n_seq)
    between = (order[None, None, :] > order[None, :, None]) & (order[None, None, :] < order[:, None, None])
    span = jnp.sum(jnp.where(between[:, :, :, None], slab_totals[None, None, :, :], 0.0), axis=2)
    earlier = (order[:, None] > order[None, :])[:, :, None]
    carry_weights = jnp.where(earlier, jnp.exp(span), 0.0)
    entering_each = jnp.sum(
        carry_weights[:, :, :, None, None] * slab_states[None], axis=1
    ).reshape(n_seq, chunk_rows, state_width)
    entering = lax.all_to_all(entering_each, "seq", 0, 0, tiled=True).reshape(
        heads, head_width, state_width
    )
    c_wide = c_rows.astype(jnp.float32)
    arriving = jnp.exp(slab_log)[:, :, None] * jnp.einsum(
        "tn,hpn->thp", c_wide, entering, precision=lax.Precision.HIGHEST
    )
    ssm_out = (
        outputs.reshape(tokens_here, heads, head_width)
        + arriving
        + skip_gain[None, :, None] * inputs.astype(jnp.float32)
    )
    gated = ssm_out.reshape(tokens_here, inner) * jax.nn.silu(gate_input.astype(jnp.float32))
    normed = (
        gated
        * lax.rsqrt(jnp.mean(gated * gated, axis=1, keepdims=True) + 1e-05)
        * norm_gain[None, :]
    ).astype(jnp.bfloat16)
    n_batch = lax.axis_size("batch")
    core = lax.axis_index("batch") % 2
    depth = w_out.shape[0] // 2
    with jax.named_scope("wgather"):
        w_rows = lax.all_gather(
            lax.dynamic_slice_in_dim(w_out, core * depth, depth, axis=0), "seq", axis=1, tiled=True
        )
    partners = [(b, b ^ 1) for b in range(n_batch)]
    own_rows = lax.dynamic_slice_in_dim(normed, core * depth, depth, axis=1)
    partner_rows = lax.ppermute(
        lax.dynamic_slice_in_dim(normed, (1 - core) * depth, depth, axis=1), "batch", partners
    )
    own_part = jnp.dot(own_rows, w_rows, preferred_element_type=jnp.float32)
    partner_part = jnp.dot(partner_rows, w_rows, preferred_element_type=jnp.float32)
    other_part = lax.ppermute(partner_part, "batch", partners)
    mixer_out = (own_part + other_part).astype(jnp.bfloat16)
    hidden = (residual.astype(jnp.float32) + mixer_out.astype(jnp.float32)).astype(jnp.bfloat16)
    hidden_wide = hidden.astype(jnp.float32)
    moe_input = (
        hidden_wide
        * lax.rsqrt(jnp.mean(hidden_wide * hidden_wide, axis=1, keepdims=True) + 1e-05)
        * moe_gain[None, :]
    ).astype(jnp.bfloat16)
    logits = jnp.dot(moe_input, router, preferred_element_type=jnp.float32)
    chosen = jnp.take_along_axis(logits, expert_ids, axis=1)
    powers = jnp.exp(chosen)
    combine = powers / jnp.sum(powers, axis=1, keepdims=True)
    experts_all = lax.axis_size("seq")
    fanout = expert_ids.shape[1]
    capacity = tokens_here * fanout * 3 // (2 * experts_all)
    width = moe_input.shape[1]
    flat_ids = expert_ids.reshape(-1)
    one_hot = (flat_ids[:, None] == jnp.arange(experts_all, dtype=jnp.int32)[None, :]).astype(
        jnp.int32
    )
    running_count = jnp.cumsum(one_hot, axis=0)
    slot_of = jnp.sum(running_count * one_hot, axis=1) - 1
    target = flat_ids * capacity + slot_of
    slots = experts_all * capacity
    target_pairs = target.reshape(tokens_here, fanout)
    slot_ids = jnp.arange(slots, dtype=jnp.int32)
    placing = jnp.zeros((slots, tokens_here), jnp.bool_)
    for k in range(fanout):
        placing = placing | (slot_ids[:, None] == target_pairs[None, :, k])
    departing_state = jnp.dot(
        placing.astype(jnp.bfloat16), moe_input, preferred_element_type=jnp.float32
    ).astype(jnp.bfloat16)
    departing_state = departing_state.reshape(experts_all, capacity, width)
    batch = lax.all_to_all(departing_state, "seq", split_axis=0, concat_axis=0, tiled=True)
    flat_rows = batch.reshape(-1, width)
    gate_part = jnp.dot(flat_rows, w_gate[0], preferred_element_type=jnp.float32)
    up_part = jnp.dot(flat_rows, w_up[0], preferred_element_type=jnp.float32)
    expert_hidden = (jax.nn.silu(gate_part) * up_part).astype(jnp.bfloat16)
    result = jnp.dot(expert_hidden, w_down[0], preferred_element_type=jnp.float32).astype(
        jnp.bfloat16
    )
    finished = result.reshape(batch.shape)
    returned = lax.all_to_all(finished, "seq", split_axis=0, concat_axis=0, tiled=True).reshape(
        experts_all * capacity, width
    )
    total = hidden_wide
    for k in range(fanout):
        picking = (target_pairs[:, k][:, None] == slot_ids[None, :]).astype(jnp.bfloat16)
        fetched = jnp.dot(picking, returned, preferred_element_type=jnp.float32)
        total = total + combine[:, k][:, None] * fetched
    return total.astype(jnp.bfloat16)


def solution(mesh):
    in_specs = (
        P(("batch", "seq"), None),
        P(("batch", "seq"), None),
        P(("batch", "seq"), None),
        P(("batch", "seq"), None),
        P(("batch", "seq"), None),
        P(),
        P(),
        P(),
        P(),
        P(None, "seq"),
        P(("batch", "seq"), None),
        P(),
        P(),
        P(("batch", "seq"), None),
        P("seq", None, None),
        P("seq", None, None),
        P("seq", None, None),
    )
    out_specs = P(("batch", "seq"), None)
    return jax.shard_map(shards, mesh=mesh, in_specs=in_specs, out_specs=out_specs, check_vma=False)
```

```python
import jax
import jax.numpy as jnp
from jax import lax
from jax.sharding import PartitionSpec as P

GROUP = 256


def group_pass(carried, pieces):
    inputs, b_block, c_block, steps_h, logs_h = pieces
    running = jnp.cumsum(logs_h, axis=0)
    length = logs_h.shape[0]
    scores = jnp.dot(c_block, b_block.T, preferred_element_type=jnp.float32)
    causal = jnp.arange(length)[:, None] >= jnp.arange(length)[None, :]
    spread = running[:, None, :] - running[None, :, :]
    decays = jnp.exp(jnp.where(causal[:, :, None], spread, -jnp.inf))
    mixing = (scores[:, :, None] * decays * steps_h[None, :, :]).astype(jnp.bfloat16)
    intra = jnp.einsum("tsh,shp->thp", mixing, inputs, preferred_element_type=jnp.float32)
    c_wide = c_block.astype(jnp.float32)
    from_state = jnp.exp(running)[:, :, None] * jnp.einsum(
        "tn,hpn->thp", c_wide, carried, precision=lax.Precision.HIGHEST
    )
    departing_state = jnp.exp(running[-1][None, :] - running) * steps_h
    block_in = (departing_state[:, :, None] * b_block.astype(jnp.float32)[:, None, :]).astype(
        jnp.bfloat16
    )
    update = jnp.einsum("shn,shp->hpn", block_in, inputs, preferred_element_type=jnp.float32)
    new_carried = jnp.exp(running[-1])[:, None, None] * carried + update
    return (new_carried, intra + from_state)


def shards(
    ssm_input,
    gate_input,
    b_rows,
    c_rows,
    step_raw,
    step_bias,
    rate_log,
    skip_gain,
    norm_gain,
    w_out,
    residual,
    moe_gain,
    router,
    expert_ids,
    w_gate,
    w_up,
    w_down,
):
    tokens_here = ssm_input.shape[0]
    inner = ssm_input.shape[1]
    heads = rate_log.shape[0]
    head_width = inner // heads
    state_width = b_rows.shape[1]
    blocks = tokens_here // GROUP
    step_sizes = jax.nn.softplus(step_raw + step_bias[None, :])
    log_decay = -step_sizes * jnp.exp(rate_log)[None, :]
    inputs = ssm_input.reshape(tokens_here, heads, head_width)
    pieces = (
        inputs.reshape(blocks, GROUP, heads, head_width),
        b_rows.reshape(blocks, GROUP, state_width),
        c_rows.reshape(blocks, GROUP, state_width),
        step_sizes.reshape(blocks, GROUP, heads),
        log_decay.reshape(blocks, GROUP, heads),
    )
    start = jnp.zeros((heads, head_width, state_width), jnp.float32)
    segment_state, outputs = lax.scan(group_pass, start, pieces)
    slab_log = jnp.cumsum(log_decay, axis=0)
    slab_total = slab_log[-1]
    n_seq = lax.axis_size("seq")
    per_chunk = heads // n_seq
    chunk_rows = per_chunk * head_width
    state_rows = segment_state.reshape(n_seq, chunk_rows, state_width)
    total_hi = slab_total.astype(jnp.bfloat16)
    rest = slab_total - total_hi.astype(jnp.float32)
    total_mid = rest.astype(jnp.bfloat16)
    total_lo = (rest - total_mid.astype(jnp.float32)).astype(jnp.bfloat16)
    total_parts = jnp.stack([total_hi, total_mid, total_lo]).reshape(3, n_seq, per_chunk)
    total_rows = jnp.broadcast_to(
        total_parts.transpose(1, 0, 2).reshape(n_seq, 3 * per_chunk, 1),
        (n_seq, 3 * per_chunk, state_width),
    )
    total_block = jnp.pad(total_rows, ((0, 0), (0, 16 - 3 * per_chunk), (0, 0)))
    packed = jnp.concatenate([state_rows.astype(jnp.bfloat16), total_block], axis=1)
    received = lax.all_to_all(packed, "seq", 0, 0, tiled=True)
    slab_states = (
        received[:, :chunk_rows].astype(jnp.float32).reshape(n_seq, per_chunk, head_width, state_width)
    )
    total_got = received[:, chunk_rows : chunk_rows + 3 * per_chunk, 0].astype(jnp.float32)
    slab_totals = (
        total_got[:, :per_chunk] + total_got[:, per_chunk : 2 * per_chunk]
    ) + total_got[:, 2 * per_chunk :]
    order = jnp.arange(n_seq)
    between = (order[None, None, :] > order[None, :, None]) & (order[None, None, :] < order[:, None, None])
    span = jnp.sum(jnp.where(between[:, :, :, None], slab_totals[None, None, :, :], 0.0), axis=2)
    earlier = (order[:, None] > order[None, :])[:, :, None]
    carry_weights = jnp.where(earlier, jnp.exp(span), 0.0)
    entering_each = jnp.sum(
        carry_weights[:, :, :, None, None] * slab_states[None], axis=1
    ).reshape(n_seq, chunk_rows, state_width)
    entering = lax.all_to_all(entering_each, "seq", 0, 0, tiled=True).reshape(
        heads, head_width, state_width
    )
    c_wide = c_rows.astype(jnp.float32)
    arriving = jnp.exp(slab_log)[:, :, None] * jnp.einsum(
        "tn,hpn->thp", c_wide, entering, precision=lax.Precision.HIGHEST
    )
    ssm_out = (
        outputs.reshape(tokens_here, heads, head_width)
        + arriving
        + skip_gain[None, :, None] * inputs.astype(jnp.float32)
    )
    gated = ssm_out.reshape(tokens_here, inner) * jax.nn.silu(gate_input.astype(jnp.float32))
    normed = (
        gated
        * lax.rsqrt(jnp.mean(gated * gated, axis=1, keepdims=True) + 1e-05)
        * norm_gain[None, :]
    ).astype(jnp.bfloat16)
    n_batch = lax.axis_size("batch")
    core = lax.axis_index("batch") % 2
    depth = w_out.shape[0] // 2
    with jax.named_scope("wgather"):
        w_rows = lax.all_gather(
            lax.dynamic_slice_in_dim(w_out, core * depth, depth, axis=0), "seq", axis=1, tiled=True
        )
    partners = [(b, b ^ 1) for b in range(n_batch)]
    own_rows = lax.dynamic_slice_in_dim(normed, core * depth, depth, axis=1)
    partner_rows = lax.ppermute(
        lax.dynamic_slice_in_dim(normed, (1 - core) * depth, depth, axis=1), "batch", partners
    )
    own_part = jnp.dot(own_rows, w_rows, preferred_element_type=jnp.float32)
    partner_part = jnp.dot(partner_rows, w_rows, preferred_element_type=jnp.float32)
    other_part = lax.ppermute(partner_part, "batch", partners)
    mixer_out = (own_part + other_part).astype(jnp.bfloat16)
    hidden = (residual.astype(jnp.float32) + mixer_out.astype(jnp.float32)).astype(jnp.bfloat16)
    hidden_wide = hidden.astype(jnp.float32)
    moe_input = (
        hidden_wide
        * lax.rsqrt(jnp.mean(hidden_wide * hidden_wide, axis=1, keepdims=True) + 1e-05)
        * moe_gain[None, :]
    ).astype(jnp.bfloat16)
    logits = jnp.dot(moe_input, router, preferred_element_type=jnp.float32)
    chosen = jnp.take_along_axis(logits, expert_ids, axis=1)
    powers = jnp.exp(chosen)
    combine = powers / jnp.sum(powers, axis=1, keepdims=True)
    experts_all = lax.axis_size("seq")
    fanout = expert_ids.shape[1]
    capacity = tokens_here * fanout * 3 // (2 * experts_all)
    width = moe_input.shape[1]
    flat_ids = expert_ids.reshape(-1)
    one_hot = (flat_ids[:, None] == jnp.arange(experts_all, dtype=jnp.int32)[None, :]).astype(
        jnp.int32
    )
    running_count = jnp.cumsum(one_hot, axis=0)
    slot_of = jnp.sum(running_count * one_hot, axis=1) - 1
    target = flat_ids * capacity + slot_of
    slots = experts_all * capacity
    target_pairs = target.reshape(tokens_here, fanout)
    slot_ids = jnp.arange(slots, dtype=jnp.int32)
    placing = jnp.zeros((slots, tokens_here), jnp.bool_)
    for k in range(fanout):
        placing = placing | (slot_ids[:, None] == target_pairs[None, :, k])
    departing_state = jnp.dot(
        placing.astype(jnp.bfloat16), moe_input, preferred_element_type=jnp.float32
    ).astype(jnp.bfloat16)
    departing_state = departing_state.reshape(experts_all, capacity, width)
    batch = lax.all_to_all(departing_state, "seq", split_axis=0, concat_axis=0, tiled=True)
    flat_rows = batch.reshape(-1, width)
    gate_part = jnp.dot(flat_rows, w_gate[0], preferred_element_type=jnp.float32)
    up_part = jnp.dot(flat_rows, w_up[0], preferred_element_type=jnp.float32)
    expert_hidden = (jax.nn.silu(gate_part) * up_part).astype(jnp.bfloat16)
    result = jnp.dot(expert_hidden, w_down[0], preferred_element_type=jnp.float32).astype(
        jnp.bfloat16
    )
    finished = result.reshape(batch.shape)
    returned = lax.all_to_all(finished, "seq", split_axis=0, concat_axis=0, tiled=True).reshape(
        experts_all * capacity, width
    )
    total = hidden_wide
    for k in range(fanout):
        picking = (target_pairs[:, k][:, None] == slot_ids[None, :]).astype(jnp.bfloat16)
        fetched = jnp.dot(picking, returned, preferred_element_type=jnp.float32)
        total = total + combine[:, k][:, None] * fetched
    return total.astype(jnp.bfloat16)


def solution(mesh):
    in_specs = (
        P(("batch", "seq"), None),
        P(("batch", "seq"), None),
        P(("batch", "seq"), None),
        P(("batch", "seq"), None),
        P(("batch", "seq"), None),
        P(),
        P(),
        P(),
        P(),
        P(None, "seq"),
        P(("batch", "seq"), None),
        P(),
        P(),
        P(("batch", "seq"), None),
        P("seq", None, None),
        P("seq", None, None),
        P("seq", None, None),
    )
    out_specs = P(("batch", "seq"), None)
    return jax.shard_map(shards, mesh=mesh, in_specs=in_specs, out_specs=out_specs, check_vma=False)
```

```python
import jax
import jax.numpy as jnp
from jax import lax
from jax.sharding import PartitionSpec as P

GROUP = 256


def group_pass(carried, pieces):
    inputs, b_block, c_block, steps_h, logs_h = pieces
    running = jnp.cumsum(logs_h, axis=0)
    length = logs_h.shape[0]
    scores = jnp.dot(c_block, b_block.T, preferred_element_type=jnp.float32)
    causal = jnp.arange(length)[:, None] >= jnp.arange(length)[None, :]
    spread = running[:, None, :] - running[None, :, :]
    decays = jnp.exp(jnp.where(causal[:, :, None], spread, -jnp.inf))
    mixing = (scores[:, :, None] * decays * steps_h[None, :, :]).astype(jnp.bfloat16)
    intra = jnp.einsum("tsh,shp->thp", mixing, inputs, preferred_element_type=jnp.float32)
    c_wide = c_block.astype(jnp.float32)
    from_state = jnp.exp(running)[:, :, None] * jnp.einsum(
        "tn,hpn->thp", c_wide, carried, precision=lax.Precision.HIGHEST
    )
    departing_state = jnp.exp(running[-1][None, :] - running) * steps_h
    block_in = (departing_state[:, :, None] * b_block.astype(jnp.float32)[:, None, :]).astype(
        jnp.bfloat16
    )
    update = jnp.einsum("shn,shp->hpn", block_in, inputs, preferred_element_type=jnp.float32)
    new_carried = jnp.exp(running[-1])[:, None, None] * carried + update
    return (new_carried, intra + from_state)


def shards(
    ssm_input,
    gate_input,
    b_rows,
    c_rows,
    step_raw,
    step_bias,
    rate_log,
    skip_gain,
    norm_gain,
    w_out,
    residual,
    moe_gain,
    router,
    expert_ids,
    w_gate,
    w_up,
    w_down,
):
    tokens_here = ssm_input.shape[0]
    inner = ssm_input.shape[1]
    heads = rate_log.shape[0]
    head_width = inner // heads
    state_width = b_rows.shape[1]
    blocks = tokens_here // GROUP
    step_sizes = jax.nn.softplus(step_raw + step_bias[None, :])
    log_decay = -step_sizes * jnp.exp(rate_log)[None, :]
    inputs = ssm_input.reshape(tokens_here, heads, head_width)
    pieces = (
        inputs.reshape(blocks, GROUP, heads, head_width),
        b_rows.reshape(blocks, GROUP, state_width),
        c_rows.reshape(blocks, GROUP, state_width),
        step_sizes.reshape(blocks, GROUP, heads),
        log_decay.reshape(blocks, GROUP, heads),
    )
    start = jnp.zeros((heads, head_width, state_width), jnp.float32)
    segment_state, outputs = lax.scan(group_pass, start, pieces)
    slab_log = jnp.cumsum(log_decay, axis=0)
    slab_total = slab_log[-1]
    n_seq = lax.axis_size("seq")
    per_chunk = heads // n_seq
    chunk_rows = per_chunk * head_width
    state_rows = segment_state.reshape(n_seq, chunk_rows, state_width)
    total_rows = jnp.broadcast_to(slab_total.reshape(n_seq, per_chunk, 1), (n_seq, per_chunk, state_width))
    total_block = jnp.pad(total_rows, ((0, 0), (0, 8 - per_chunk), (0, 0)))
    packed = jnp.concatenate([state_rows, total_block], axis=1)
    received = lax.all_to_all(packed, "seq", 0, 0, tiled=True)
    slab_states = received[:, :chunk_rows].reshape(n_seq, per_chunk, head_width, state_width)
    slab_totals = received[:, chunk_rows : chunk_rows + per_chunk, 0]
    order = jnp.arange(n_seq)
    between = (order[None, None, :] > order[None, :, None]) & (order[None, None, :] < order[:, None, None])
    span = jnp.sum(jnp.where(between[:, :, :, None], slab_totals[None, None, :, :], 0.0), axis=2)
    earlier = (order[:, None] > order[None, :])[:, :, None]
    carry_weights = jnp.where(earlier, jnp.exp(span), 0.0)
    entering_each = jnp.sum(
        carry_weights[:, :, :, None, None] * slab_states[None], axis=1
    ).reshape(n_seq, chunk_rows, state_width)
    entering = lax.all_to_all(entering_each, "seq", 0, 0, tiled=True).reshape(
        heads, head_width, state_width
    )
    c_wide = c_rows.astype(jnp.float32)
    arriving = jnp.exp(slab_log)[:, :, None] * jnp.einsum(
        "tn,hpn->thp", c_wide, entering, precision=lax.Precision.HIGHEST
    )
    ssm_out = (
        outputs.reshape(tokens_here, heads, head_width)
        + arriving
        + skip_gain[None, :, None] * inputs.astype(jnp.float32)
    )
    gated = ssm_out.reshape(tokens_here, inner) * jax.nn.silu(gate_input.astype(jnp.float32))
    normed = (
        gated
        * lax.rsqrt(jnp.mean(gated * gated, axis=1, keepdims=True) + 1e-05)
        * norm_gain[None, :]
    ).astype(jnp.bfloat16)
    n_batch = lax.axis_size("batch")
    core = lax.axis_index("batch") % 2
    depth = w_out.shape[0] // 2
    with jax.named_scope("wgather"):
        w_rows = lax.all_gather(
            lax.dynamic_slice_in_dim(w_out, core * depth, depth, axis=0), "seq", axis=1, tiled=True
        )
    partners = [(b, b ^ 1) for b in range(n_batch)]
    own_rows = lax.dynamic_slice_in_dim(normed, core * depth, depth, axis=1)
    partner_rows = lax.ppermute(
        lax.dynamic_slice_in_dim(normed, (1 - core) * depth, depth, axis=1), "batch", partners
    )
    own_part = jnp.dot(own_rows, w_rows, preferred_element_type=jnp.float32)
    partner_part = jnp.dot(partner_rows, w_rows, preferred_element_type=jnp.float32)
    other_part = lax.ppermute(partner_part, "batch", partners)
    mixer_out = (own_part + other_part).astype(jnp.bfloat16)
    hidden = (residual.astype(jnp.float32) + mixer_out.astype(jnp.float32)).astype(jnp.bfloat16)
    hidden_wide = hidden.astype(jnp.float32)
    moe_input = (
        hidden_wide
        * lax.rsqrt(jnp.mean(hidden_wide * hidden_wide, axis=1, keepdims=True) + 1e-05)
        * moe_gain[None, :]
    ).astype(jnp.bfloat16)
    logits = jnp.dot(moe_input, router, preferred_element_type=jnp.float32)
    chosen = jnp.take_along_axis(logits, expert_ids, axis=1)
    powers = jnp.exp(chosen)
    combine = powers / jnp.sum(powers, axis=1, keepdims=True)
    experts_all = lax.axis_size("seq")
    fanout = expert_ids.shape[1]
    capacity = tokens_here * fanout * 3 // (2 * experts_all)
    width = moe_input.shape[1]
    flat_ids = expert_ids.reshape(-1)
    one_hot = (flat_ids[:, None] == jnp.arange(experts_all, dtype=jnp.int32)[None, :]).astype(
        jnp.int32
    )
    running_count = jnp.cumsum(one_hot, axis=0)
    slot_of = jnp.sum(running_count * one_hot, axis=1) - 1
    target = flat_ids * capacity + slot_of
    slots = experts_all * capacity
    target_pairs = target.reshape(tokens_here, fanout)
    slot_ids = jnp.arange(slots, dtype=jnp.int32)
    placing = jnp.zeros((slots, tokens_here), jnp.bool_)
    for k in range(fanout):
        placing = placing | (slot_ids[:, None] == target_pairs[None, :, k])
    departing_state = jnp.dot(
        placing.astype(jnp.bfloat16), moe_input, preferred_element_type=jnp.float32
    ).astype(jnp.bfloat16)
    departing_state = departing_state.reshape(experts_all, capacity, width)
    batch = lax.all_to_all(departing_state, "seq", split_axis=0, concat_axis=0, tiled=True)
    flat_rows = batch.reshape(-1, width)
    gate_part = jnp.dot(flat_rows, w_gate[0], preferred_element_type=jnp.float32)
    up_part = jnp.dot(flat_rows, w_up[0], preferred_element_type=jnp.float32)
    expert_hidden = (jax.nn.silu(gate_part) * up_part).astype(jnp.bfloat16)
    result = jnp.dot(expert_hidden, w_down[0], preferred_element_type=jnp.float32).astype(
        jnp.bfloat16
    )
    finished = result.reshape(batch.shape)
    returned = lax.all_to_all(finished, "seq", split_axis=0, concat_axis=0, tiled=True).reshape(
        experts_all * capacity, width
    )
    picking = (target_pairs.T.reshape(-1)[:, None] == slot_ids[None, :]).astype(jnp.bfloat16)
    fetched = jnp.dot(picking, returned, preferred_element_type=jnp.float32).reshape(
        fanout, tokens_here, width
    )
    total = hidden_wide
    for k in range(fanout):
        total = total + combine[:, k][:, None] * fetched[k]
    return total.astype(jnp.bfloat16)


def solution(mesh):
    in_specs = (
        P(("batch", "seq"), None),
        P(("batch", "seq"), None),
        P(("batch", "seq"), None),
        P(("batch", "seq"), None),
        P(("batch", "seq"), None),
        P(),
        P(),
        P(),
        P(),
        P(None, "seq"),
        P(("batch", "seq"), None),
        P(),
        P(),
        P(("batch", "seq"), None),
        P("seq", None, None),
        P("seq", None, None),
        P("seq", None, None),
    )
    out_specs = P(("batch", "seq"), None)
    return jax.shard_map(shards, mesh=mesh, in_specs=in_specs, out_specs=out_specs, check_vma=False)
```

```python
import jax
import jax.numpy as jnp
from jax import lax
from jax.sharding import PartitionSpec as P

GROUP = 256


def group_pass(carried, pieces):
    inputs, b_block, c_block, steps_h, logs_h = pieces
    running = jnp.cumsum(logs_h, axis=0)
    length = logs_h.shape[0]
    scores = jnp.dot(c_block, b_block.T, preferred_element_type=jnp.float32)
    causal = jnp.arange(length)[:, None] >= jnp.arange(length)[None, :]
    spread = running[:, None, :] - running[None, :, :]
    decays = jnp.exp(jnp.where(causal[:, :, None], spread, -jnp.inf))
    mixing = (scores[:, :, None] * decays * steps_h[None, :, :]).astype(jnp.bfloat16)
    intra = jnp.einsum("tsh,shp->thp", mixing, inputs, preferred_element_type=jnp.float32)
    c_wide = c_block.astype(jnp.float32)
    from_state = jnp.exp(running)[:, :, None] * jnp.einsum(
        "tn,hpn->thp", c_wide, carried, precision=lax.Precision.HIGHEST
    )
    departing_state = jnp.exp(running[-1][None, :] - running) * steps_h
    block_in = (departing_state[:, :, None] * b_block.astype(jnp.float32)[:, None, :]).astype(
        jnp.bfloat16
    )
    update = jnp.einsum("shn,shp->hpn", block_in, inputs, preferred_element_type=jnp.float32)
    new_carried = jnp.exp(running[-1])[:, None, None] * carried + update
    return (new_carried, intra + from_state)


def shards(
    ssm_input,
    gate_input,
    b_rows,
    c_rows,
    step_raw,
    step_bias,
    rate_log,
    skip_gain,
    norm_gain,
    w_out,
    residual,
    moe_gain,
    router,
    expert_ids,
    w_gate,
    w_up,
    w_down,
):
    tokens_here = ssm_input.shape[0]
    inner = ssm_input.shape[1]
    heads = rate_log.shape[0]
    head_width = inner // heads
    state_width = b_rows.shape[1]
    blocks = tokens_here // GROUP
    step_sizes = jax.nn.softplus(step_raw + step_bias[None, :])
    log_decay = -step_sizes * jnp.exp(rate_log)[None, :]
    inputs = ssm_input.reshape(tokens_here, heads, head_width)
    pieces = (
        inputs.reshape(blocks, GROUP, heads, head_width),
        b_rows.reshape(blocks, GROUP, state_width),
        c_rows.reshape(blocks, GROUP, state_width),
        step_sizes.reshape(blocks, GROUP, heads),
        log_decay.reshape(blocks, GROUP, heads),
    )
    start = jnp.zeros((heads, head_width, state_width), jnp.float32)
    segment_state, outputs = lax.scan(group_pass, start, pieces)
    slab_log = jnp.cumsum(log_decay, axis=0)
    slab_total = slab_log[-1]
    n_seq = lax.axis_size("seq")
    per_chunk = heads // n_seq
    chunk_rows = per_chunk * head_width
    state_rows = segment_state.reshape(n_seq, chunk_rows, state_width)
    total_rows = jnp.broadcast_to(slab_total.reshape(n_seq, per_chunk, 1), (n_seq, per_chunk, state_width))
    total_block = jnp.pad(total_rows, ((0, 0), (0, 8 - per_chunk), (0, 0)))
    packed = jnp.concatenate([state_rows, total_block], axis=1)
    received = lax.all_to_all(packed, "seq", 0, 0, tiled=True)
    slab_states = received[:, :chunk_rows].reshape(n_seq, per_chunk, head_width, state_width)
    slab_totals = received[:, chunk_rows : chunk_rows + per_chunk, 0]
    order = jnp.arange(n_seq)
    between = (order[None, None, :] > order[None, :, None]) & (order[None, None, :] < order[:, None, None])
    span = jnp.sum(jnp.where(between[:, :, :, None], slab_totals[None, None, :, :], 0.0), axis=2)
    earlier = (order[:, None] > order[None, :])[:, :, None]
    carry_weights = jnp.where(earlier, jnp.exp(span), 0.0)
    entering_each = jnp.sum(
        carry_weights[:, :, :, None, None] * slab_states[None], axis=1
    ).reshape(n_seq, chunk_rows, state_width)
    entering = lax.all_to_all(entering_each, "seq", 0, 0, tiled=True).reshape(
        heads, head_width, state_width
    )
    c_wide = c_rows.astype(jnp.float32)
    arriving = jnp.exp(slab_log)[:, :, None] * jnp.einsum(
        "tn,hpn->thp", c_wide, entering, precision=lax.Precision.HIGHEST
    )
    ssm_out = (
        outputs.reshape(tokens_here, heads, head_width)
        + arriving
        + skip_gain[None, :, None] * inputs.astype(jnp.float32)
    )
    gated = ssm_out.reshape(tokens_here, inner) * jax.nn.silu(gate_input.astype(jnp.float32))
    normed = (
        gated
        * lax.rsqrt(jnp.mean(gated * gated, axis=1, keepdims=True) + 1e-05)
        * norm_gain[None, :]
    ).astype(jnp.bfloat16)
    n_batch = lax.axis_size("batch")
    core = lax.axis_index("batch") % 2
    depth = w_out.shape[0] // 2
    with jax.named_scope("wgather"):
        w_rows = lax.all_gather(
            lax.dynamic_slice_in_dim(w_out, core * depth, depth, axis=0), "seq", axis=1, tiled=True
        )
    partners = [(b, b ^ 1) for b in range(n_batch)]
    own_rows = lax.dynamic_slice_in_dim(normed, core * depth, depth, axis=1)
    partner_rows = lax.ppermute(
        lax.dynamic_slice_in_dim(normed, (1 - core) * depth, depth, axis=1), "batch", partners
    )
    own_part = jnp.dot(own_rows, w_rows, preferred_element_type=jnp.float32)
    partner_part = jnp.dot(partner_rows, w_rows, preferred_element_type=jnp.float32)
    other_part = lax.ppermute(partner_part, "batch", partners)
    mixer_out = (own_part + other_part).astype(jnp.bfloat16)
    hidden = (residual.astype(jnp.float32) + mixer_out.astype(jnp.float32)).astype(jnp.bfloat16)
    hidden_wide = hidden.astype(jnp.float32)
    moe_input = (
        hidden_wide
        * lax.rsqrt(jnp.mean(hidden_wide * hidden_wide, axis=1, keepdims=True) + 1e-05)
        * moe_gain[None, :]
    ).astype(jnp.bfloat16)
    logits = jnp.dot(moe_input, router, preferred_element_type=jnp.float32)
    chosen = jnp.take_along_axis(logits, expert_ids, axis=1)
    powers = jnp.exp(chosen)
    combine = powers / jnp.sum(powers, axis=1, keepdims=True)
    experts_all = lax.axis_size("seq")
    fanout = expert_ids.shape[1]
    capacity = tokens_here * fanout * 3 // (2 * experts_all)
    width = moe_input.shape[1]
    flat_ids = expert_ids.reshape(-1)
    one_hot = (flat_ids[:, None] == jnp.arange(experts_all, dtype=jnp.int32)[None, :]).astype(
        jnp.int32
    )
    running_count = jnp.cumsum(one_hot, axis=0)
    slot_of = jnp.sum(running_count * one_hot, axis=1) - 1
    target = flat_ids * capacity + slot_of
    slots = experts_all * capacity
    target_pairs = target.reshape(tokens_here, fanout)
    slot_ids = jnp.arange(slots, dtype=jnp.int32)
    placing = jnp.zeros((slots, tokens_here), jnp.bool_)
    for k in range(fanout):
        placing = placing | (slot_ids[:, None] == target_pairs[None, :, k])
    departing_state = jnp.dot(
        placing.astype(jnp.bfloat16), moe_input, preferred_element_type=jnp.float32
    ).astype(jnp.bfloat16)
    departing_state = departing_state.reshape(experts_all, capacity, width)
    batch = lax.all_to_all(departing_state, "seq", split_axis=0, concat_axis=0, tiled=True)
    flat_rows = batch.reshape(-1, width)
    hidden_units = w_gate.shape[2]
    both_proj = jnp.dot(
        flat_rows,
        jnp.concatenate([w_gate[0], w_up[0]], axis=1),
        preferred_element_type=jnp.float32,
    )
    gate_part = both_proj[:, :hidden_units]
    up_part = both_proj[:, hidden_units:]
    expert_hidden = (jax.nn.silu(gate_part) * up_part).astype(jnp.bfloat16)
    result = jnp.dot(expert_hidden, w_down[0], preferred_element_type=jnp.float32).astype(
        jnp.bfloat16
    )
    finished = result.reshape(batch.shape)
    returned = lax.all_to_all(finished, "seq", split_axis=0, concat_axis=0, tiled=True).reshape(
        experts_all * capacity, width
    )
    picking = (target_pairs.T.reshape(-1)[:, None] == slot_ids[None, :]).astype(jnp.bfloat16)
    fetched = jnp.dot(picking, returned, preferred_element_type=jnp.float32).reshape(
        fanout, tokens_here, width
    )
    total = hidden_wide
    for k in range(fanout):
        total = total + combine[:, k][:, None] * fetched[k]
    return total.astype(jnp.bfloat16)


def solution(mesh):
    in_specs = (
        P(("batch", "seq"), None),
        P(("batch", "seq"), None),
        P(("batch", "seq"), None),
        P(("batch", "seq"), None),
        P(("batch", "seq"), None),
        P(),
        P(),
        P(),
        P(),
        P(None, "seq"),
        P(("batch", "seq"), None),
        P(),
        P(),
        P(("batch", "seq"), None),
        P("seq", None, None),
        P("seq", None, None),
        P("seq", None, None),
    )
    out_specs = P(("batch", "seq"), None)
    return jax.shard_map(shards, mesh=mesh, in_specs=in_specs, out_specs=out_specs, check_vma=False)
```

```python
import jax
import jax.numpy as jnp
from jax import lax
from jax.sharding import PartitionSpec as P

GROUP = 256


def group_pass(carried, pieces):
    inputs, b_block, c_block, steps_h, logs_h = pieces
    running = jnp.cumsum(logs_h, axis=0)
    length = logs_h.shape[0]
    scores = jnp.dot(c_block, b_block.T, preferred_element_type=jnp.float32)
    causal = jnp.arange(length)[:, None] >= jnp.arange(length)[None, :]
    spread = running[:, None, :] - running[None, :, :]
    decays = jnp.exp(jnp.where(causal[:, :, None], spread, -jnp.inf))
    mixing = (scores[:, :, None] * decays * steps_h[None, :, :]).astype(jnp.bfloat16)
    intra = jnp.einsum("tsh,shp->thp", mixing, inputs, preferred_element_type=jnp.float32)
    c_wide = c_block.astype(jnp.float32)
    from_state = jnp.exp(running)[:, :, None] * jnp.einsum(
        "tn,hpn->thp", c_wide, carried, precision=lax.Precision.HIGHEST
    )
    departing_state = jnp.exp(running[-1][None, :] - running) * steps_h
    block_in = (departing_state[:, :, None] * b_block.astype(jnp.float32)[:, None, :]).astype(
        jnp.bfloat16
    )
    update = jnp.einsum("shn,shp->hpn", block_in, inputs, preferred_element_type=jnp.float32)
    new_carried = jnp.exp(running[-1])[:, None, None] * carried + update
    return (new_carried, intra + from_state)


def shards(
    ssm_input,
    gate_input,
    b_rows,
    c_rows,
    step_raw,
    step_bias,
    rate_log,
    skip_gain,
    norm_gain,
    w_out,
    residual,
    moe_gain,
    router,
    expert_ids,
    w_gate,
    w_up,
    w_down,
):
    tokens_here = ssm_input.shape[0]
    inner = ssm_input.shape[1]
    heads = rate_log.shape[0]
    head_width = inner // heads
    state_width = b_rows.shape[1]
    blocks = tokens_here // GROUP
    step_sizes = jax.nn.softplus(step_raw + step_bias[None, :])
    log_decay = -step_sizes * jnp.exp(rate_log)[None, :]
    inputs = ssm_input.reshape(tokens_here, heads, head_width)
    pieces = (
        inputs.reshape(blocks, GROUP, heads, head_width),
        b_rows.reshape(blocks, GROUP, state_width),
        c_rows.reshape(blocks, GROUP, state_width),
        step_sizes.reshape(blocks, GROUP, heads),
        log_decay.reshape(blocks, GROUP, heads),
    )
    start = jnp.zeros((heads, head_width, state_width), jnp.float32)
    segment_state, outputs = lax.scan(group_pass, start, pieces)
    slab_log = jnp.cumsum(log_decay, axis=0)
    slab_total = slab_log[-1]
    n_seq = lax.axis_size("seq")
    per_chunk = heads // n_seq
    chunk_rows = per_chunk * head_width
    state_rows = segment_state.reshape(n_seq, chunk_rows, state_width)
    total_rows = jnp.broadcast_to(slab_total.reshape(n_seq, per_chunk, 1), (n_seq, per_chunk, state_width))
    total_block = jnp.pad(total_rows, ((0, 0), (0, 8 - per_chunk), (0, 0)))
    packed = jnp.concatenate([state_rows, total_block], axis=1)
    received = lax.all_to_all(packed, "seq", 0, 0, tiled=True)
    slab_states = received[:, :chunk_rows].reshape(n_seq, per_chunk, head_width, state_width)
    slab_totals = received[:, chunk_rows : chunk_rows + per_chunk, 0]
    order = jnp.arange(n_seq)
    between = (order[None, None, :] > order[None, :, None]) & (order[None, None, :] < order[:, None, None])
    span = jnp.sum(jnp.where(between[:, :, :, None], slab_totals[None, None, :, :], 0.0), axis=2)
    earlier = (order[:, None] > order[None, :])[:, :, None]
    carry_weights = jnp.where(earlier, jnp.exp(span), 0.0)
    entering_each = jnp.sum(
        carry_weights[:, :, :, None, None] * slab_states[None], axis=1
    ).reshape(n_seq, chunk_rows, state_width)
    entering = lax.all_to_all(entering_each, "seq", 0, 0, tiled=True).reshape(
        heads, head_width, state_width
    )
    c_wide = c_rows.astype(jnp.float32)
    arriving = jnp.exp(slab_log)[:, :, None] * jnp.einsum(
        "tn,hpn->thp", c_wide, entering, precision=lax.Precision.HIGHEST
    )
    ssm_out = (
        outputs.reshape(tokens_here, heads, head_width)
        + arriving
        + skip_gain[None, :, None] * inputs.astype(jnp.float32)
    )
    gated = ssm_out.reshape(tokens_here, inner) * jax.nn.silu(gate_input.astype(jnp.float32))
    normed = (
        gated
        * lax.rsqrt(jnp.mean(gated * gated, axis=1, keepdims=True) + 1e-05)
        * norm_gain[None, :]
    ).astype(jnp.bfloat16)
    n_batch = lax.axis_size("batch")
    core = lax.axis_index("batch") % 2
    depth = w_out.shape[0] // 2
    with jax.named_scope("wgather"):
        w_rows = lax.all_gather(
            jnp.where(core == 0, w_out[:depth], w_out[depth:]), "seq", axis=1, tiled=True
        )
    partners = [(b, b ^ 1) for b in range(n_batch)]
    own_rows = lax.dynamic_slice_in_dim(normed, core * depth, depth, axis=1)
    partner_rows = lax.ppermute(
        lax.dynamic_slice_in_dim(normed, (1 - core) * depth, depth, axis=1), "batch", partners
    )
    own_part = jnp.dot(own_rows, w_rows, preferred_element_type=jnp.float32)
    partner_part = jnp.dot(partner_rows, w_rows, preferred_element_type=jnp.float32)
    other_part = lax.ppermute(partner_part, "batch", partners)
    mixer_out = (own_part + other_part).astype(jnp.bfloat16)
    hidden = (residual.astype(jnp.float32) + mixer_out.astype(jnp.float32)).astype(jnp.bfloat16)
    hidden_wide = hidden.astype(jnp.float32)
    moe_input = (
        hidden_wide
        * lax.rsqrt(jnp.mean(hidden_wide * hidden_wide, axis=1, keepdims=True) + 1e-05)
        * moe_gain[None, :]
    ).astype(jnp.bfloat16)
    logits = jnp.dot(moe_input, router, preferred_element_type=jnp.float32)
    chosen = jnp.take_along_axis(logits, expert_ids, axis=1)
    powers = jnp.exp(chosen)
    combine = powers / jnp.sum(powers, axis=1, keepdims=True)
    experts_all = lax.axis_size("seq")
    fanout = expert_ids.shape[1]
    capacity = tokens_here * fanout * 3 // (2 * experts_all)
    width = moe_input.shape[1]
    flat_ids = expert_ids.reshape(-1)
    one_hot = (flat_ids[:, None] == jnp.arange(experts_all, dtype=jnp.int32)[None, :]).astype(
        jnp.int32
    )
    running_count = jnp.cumsum(one_hot, axis=0)
    slot_of = jnp.sum(running_count * one_hot, axis=1) - 1
    target = flat_ids * capacity + slot_of
    slots = experts_all * capacity
    target_pairs = target.reshape(tokens_here, fanout)
    slot_ids = jnp.arange(slots, dtype=jnp.int32)
    placing = jnp.zeros((slots, tokens_here), jnp.bool_)
    for k in range(fanout):
        placing = placing | (slot_ids[:, None] == target_pairs[None, :, k])
    departing_state = jnp.dot(
        placing.astype(jnp.bfloat16), moe_input, preferred_element_type=jnp.float32
    ).astype(jnp.bfloat16)
    departing_state = departing_state.reshape(experts_all, capacity, width)
    batch = lax.all_to_all(departing_state, "seq", split_axis=0, concat_axis=0, tiled=True)
    flat_rows = batch.reshape(-1, width)
    hidden_units = w_gate.shape[2]
    both_proj = jnp.dot(
        flat_rows,
        jnp.concatenate([w_gate[0], w_up[0]], axis=1),
        preferred_element_type=jnp.float32,
    )
    gate_part = both_proj[:, :hidden_units]
    up_part = both_proj[:, hidden_units:]
    expert_hidden = (jax.nn.silu(gate_part) * up_part).astype(jnp.bfloat16)
    result = jnp.dot(expert_hidden, w_down[0], preferred_element_type=jnp.float32).astype(
        jnp.bfloat16
    )
    finished = result.reshape(batch.shape)
    returned = lax.all_to_all(finished, "seq", split_axis=0, concat_axis=0, tiled=True).reshape(
        experts_all * capacity, width
    )
    picking = (target_pairs.T.reshape(-1)[:, None] == slot_ids[None, :]).astype(jnp.bfloat16)
    fetched = jnp.dot(picking, returned, preferred_element_type=jnp.float32).reshape(
        fanout, tokens_here, width
    )
    total = hidden_wide
    for k in range(fanout):
        total = total + combine[:, k][:, None] * fetched[k]
    return total.astype(jnp.bfloat16)


def solution(mesh):
    in_specs = (
        P(("batch", "seq"), None),
        P(("batch", "seq"), None),
        P(("batch", "seq"), None),
        P(("batch", "seq"), None),
        P(("batch", "seq"), None),
        P(),
        P(),
        P(),
        P(),
        P(None, "seq"),
        P(("batch", "seq"), None),
        P(),
        P(),
        P(("batch", "seq"), None),
        P("seq", None, None),
        P("seq", None, None),
        P("seq", None, None),
    )
    out_specs = P(("batch", "seq"), None)
    return jax.shard_map(shards, mesh=mesh, in_specs=in_specs, out_specs=out_specs, check_vma=False)
```

```python
import jax
import jax.numpy as jnp
from jax import lax
from jax.sharding import PartitionSpec as P

GROUP = 256


def group_pass(carried, pieces):
    inputs, b_block, c_block, steps_h, logs_h = pieces
    running = jnp.cumsum(logs_h, axis=0)
    length = logs_h.shape[0]
    scores = jnp.dot(c_block, b_block.T, preferred_element_type=jnp.float32)
    causal = jnp.arange(length)[:, None] >= jnp.arange(length)[None, :]
    spread = running[:, None, :] - running[None, :, :]
    decays = jnp.exp(jnp.where(causal[:, :, None], spread, -jnp.inf))
    mixing = (scores[:, :, None] * decays * steps_h[None, :, :]).astype(jnp.bfloat16)
    intra = jnp.einsum("tsh,shp->thp", mixing, inputs, preferred_element_type=jnp.float32)
    c_wide = c_block.astype(jnp.float32)
    from_state = jnp.exp(running)[:, :, None] * jnp.einsum(
        "tn,hpn->thp", c_wide, carried, precision=lax.Precision.HIGHEST
    )
    departing_state = jnp.exp(running[-1][None, :] - running) * steps_h
    block_in = (departing_state[:, :, None] * b_block.astype(jnp.float32)[:, None, :]).astype(
        jnp.bfloat16
    )
    update = jnp.einsum("shn,shp->hpn", block_in, inputs, preferred_element_type=jnp.float32)
    new_carried = jnp.exp(running[-1])[:, None, None] * carried + update
    return (new_carried, intra + from_state)


def shards(
    ssm_input,
    gate_input,
    b_rows,
    c_rows,
    step_raw,
    step_bias,
    rate_log,
    skip_gain,
    norm_gain,
    w_out,
    residual,
    moe_gain,
    router,
    expert_ids,
    w_gate,
    w_up,
    w_down,
):
    tokens_here = ssm_input.shape[0]
    inner = ssm_input.shape[1]
    heads = rate_log.shape[0]
    head_width = inner // heads
    state_width = b_rows.shape[1]
    blocks = tokens_here // GROUP
    step_sizes = jax.nn.softplus(step_raw + step_bias[None, :])
    log_decay = -step_sizes * jnp.exp(rate_log)[None, :]
    inputs = ssm_input.reshape(tokens_here, heads, head_width)
    pieces = (
        inputs.reshape(blocks, GROUP, heads, head_width),
        b_rows.reshape(blocks, GROUP, state_width),
        c_rows.reshape(blocks, GROUP, state_width),
        step_sizes.reshape(blocks, GROUP, heads),
        log_decay.reshape(blocks, GROUP, heads),
    )
    start = jnp.zeros((heads, head_width, state_width), jnp.float32)
    segment_state, outputs = lax.scan(group_pass, start, pieces)
    slab_log = jnp.cumsum(log_decay, axis=0)
    slab_total = slab_log[-1]
    n_seq = lax.axis_size("seq")
    per_chunk = heads // n_seq
    chunk_rows = per_chunk * head_width
    state_rows = segment_state.reshape(n_seq, chunk_rows, state_width)
    total_rows = jnp.broadcast_to(slab_total.reshape(n_seq, per_chunk, 1), (n_seq, per_chunk, state_width))
    total_block = jnp.pad(total_rows, ((0, 0), (0, 8 - per_chunk), (0, 0)))
    packed = jnp.concatenate([state_rows, total_block], axis=1)
    received = lax.all_to_all(packed, "seq", 0, 0, tiled=True)
    slab_states = received[:, :chunk_rows].reshape(n_seq, per_chunk, head_width, state_width)
    slab_totals = received[:, chunk_rows : chunk_rows + per_chunk, 0]
    order = jnp.arange(n_seq)
    between = (order[None, None, :] > order[None, :, None]) & (order[None, None, :] < order[:, None, None])
    span = jnp.sum(jnp.where(between[:, :, :, None], slab_totals[None, None, :, :], 0.0), axis=2)
    earlier = (order[:, None] > order[None, :])[:, :, None]
    carry_weights = jnp.where(earlier, jnp.exp(span), 0.0)
    entering_each = jnp.sum(
        carry_weights[:, :, :, None, None] * slab_states[None], axis=1
    ).reshape(n_seq, chunk_rows, state_width)
    entering = lax.all_to_all(entering_each, "seq", 0, 0, tiled=True).reshape(
        heads, head_width, state_width
    )
    c_wide = c_rows.astype(jnp.float32)
    arriving = jnp.exp(slab_log)[:, :, None] * jnp.einsum(
        "tn,hpn->thp", c_wide, entering, precision=lax.Precision.HIGHEST
    )
    ssm_out = (
        outputs.reshape(tokens_here, heads, head_width)
        + arriving
        + skip_gain[None, :, None] * inputs.astype(jnp.float32)
    )
    gated = ssm_out.reshape(tokens_here, inner) * jax.nn.silu(gate_input.astype(jnp.float32))
    normed = (
        gated
        * lax.rsqrt(jnp.mean(gated * gated, axis=1, keepdims=True) + 1e-05)
        * norm_gain[None, :]
    ).astype(jnp.bfloat16)
    n_batch = lax.axis_size("batch")
    core = lax.axis_index("batch") % 2
    depth = w_out.shape[0] // 2
    with jax.named_scope("wgather"):
        w_rows = lax.all_gather(
            lax.dynamic_slice_in_dim(w_out, core * depth, depth, axis=0), "seq", axis=1, tiled=True
        )
    partners = [(b, b ^ 1) for b in range(n_batch)]
    own_rows = lax.dynamic_slice_in_dim(normed, core * depth, depth, axis=1)
    partner_rows = lax.ppermute(
        lax.dynamic_slice_in_dim(normed, (1 - core) * depth, depth, axis=1), "batch", partners
    )
    own_part = jnp.dot(own_rows, w_rows, preferred_element_type=jnp.float32)
    partner_part = jnp.dot(partner_rows, w_rows, preferred_element_type=jnp.float32)
    other_part = lax.ppermute(partner_part, "batch", partners)
    mixer_out = (own_part + other_part).astype(jnp.bfloat16)
    hidden = (residual.astype(jnp.float32) + mixer_out.astype(jnp.float32)).astype(jnp.bfloat16)
    hidden_wide = hidden.astype(jnp.float32)
    moe_input = (
        hidden_wide
        * lax.rsqrt(jnp.mean(hidden_wide * hidden_wide, axis=1, keepdims=True) + 1e-05)
        * moe_gain[None, :]
    ).astype(jnp.bfloat16)
    logits = jnp.dot(moe_input, router, preferred_element_type=jnp.float32)
    chosen = jnp.take_along_axis(logits, expert_ids, axis=1)
    powers = jnp.exp(chosen)
    combine = powers / jnp.sum(powers, axis=1, keepdims=True)
    experts_all = lax.axis_size("seq")
    fanout = expert_ids.shape[1]
    capacity = tokens_here * fanout * 3 // (2 * experts_all)
    width = moe_input.shape[1]
    flat_ids = expert_ids.reshape(-1)
    one_hot = (flat_ids[:, None] == jnp.arange(experts_all, dtype=jnp.int32)[None, :]).astype(
        jnp.int32
    )
    running_count = jnp.cumsum(one_hot, axis=0)
    slot_of = jnp.sum(running_count * one_hot, axis=1) - 1
    target = flat_ids * capacity + slot_of
    slots = experts_all * capacity
    target_pairs = target.reshape(tokens_here, fanout)
    slot_ids = jnp.arange(slots, dtype=jnp.int32)
    placing = jnp.zeros((slots, tokens_here), jnp.bool_)
    for k in range(fanout):
        placing = placing | (slot_ids[:, None] == target_pairs[None, :, k])
    departing_state = jnp.dot(
        placing.astype(jnp.bfloat16), moe_input, preferred_element_type=jnp.float32
    ).astype(jnp.bfloat16)
    departing_state = departing_state.reshape(experts_all, capacity, width)
    batch = lax.all_to_all(departing_state, "seq", split_axis=0, concat_axis=0, tiled=True)
    flat_rows = batch.reshape(-1, width)
    hidden_units = w_gate.shape[2]
    both_proj = jnp.dot(
        flat_rows,
        jnp.concatenate([w_gate[0], w_up[0]], axis=1),
        preferred_element_type=jnp.float32,
    )
    gate_part = both_proj[:, :hidden_units]
    up_part = both_proj[:, hidden_units:]
    expert_hidden = (jax.nn.silu(gate_part) * up_part).astype(jnp.bfloat16)
    result = jnp.dot(expert_hidden, w_down[0], preferred_element_type=jnp.float32).astype(
        jnp.bfloat16
    )
    finished = result.reshape(batch.shape)
    returned = lax.all_to_all(finished, "seq", split_axis=0, concat_axis=0, tiled=True).reshape(
        experts_all * capacity, width
    )
    picking = (target_pairs.T.reshape(-1)[:, None] == slot_ids[None, :]).astype(jnp.bfloat16)
    fetched = (
        jnp.dot(picking, returned, preferred_element_type=jnp.float32)
        .astype(jnp.bfloat16)
        .reshape(fanout, tokens_here, width)
    )
    total = hidden_wide
    for k in range(fanout):
        total = total + combine[:, k][:, None] * fetched[k].astype(jnp.float32)
    return total.astype(jnp.bfloat16)


def solution(mesh):
    in_specs = (
        P(("batch", "seq"), None),
        P(("batch", "seq"), None),
        P(("batch", "seq"), None),
        P(("batch", "seq"), None),
        P(("batch", "seq"), None),
        P(),
        P(),
        P(),
        P(),
        P(None, "seq"),
        P(("batch", "seq"), None),
        P(),
        P(),
        P(("batch", "seq"), None),
        P("seq", None, None),
        P("seq", None, None),
        P("seq", None, None),
    )
    out_specs = P(("batch", "seq"), None)
    return jax.shard_map(shards, mesh=mesh, in_specs=in_specs, out_specs=out_specs, check_vma=False)
```

```python
import jax
import jax.numpy as jnp
from jax import lax
from jax.sharding import PartitionSpec as P

GROUP = 256


def group_pass(carried, pieces):
    inputs, b_block, c_block, steps_h, logs_h = pieces
    running = jnp.cumsum(logs_h, axis=0)
    length = logs_h.shape[0]
    scores = jnp.dot(c_block, b_block.T, preferred_element_type=jnp.float32)
    causal = jnp.arange(length)[:, None] >= jnp.arange(length)[None, :]
    spread = running[:, None, :] - running[None, :, :]
    decays = jnp.exp(jnp.where(causal[:, :, None], spread, -jnp.inf))
    mixing = (scores[:, :, None] * decays * steps_h[None, :, :]).astype(jnp.bfloat16)
    intra = jnp.einsum("tsh,shp->thp", mixing, inputs, preferred_element_type=jnp.float32)
    c_wide = c_block.astype(jnp.float32)
    from_state = jnp.exp(running)[:, :, None] * jnp.einsum(
        "tn,hpn->thp", c_wide, carried, precision=lax.Precision.HIGHEST
    )
    departing_state = jnp.exp(running[-1][None, :] - running) * steps_h
    block_in = (departing_state[:, :, None] * b_block.astype(jnp.float32)[:, None, :]).astype(
        jnp.bfloat16
    )
    update = jnp.einsum("shn,shp->hpn", block_in, inputs, preferred_element_type=jnp.float32)
    new_carried = jnp.exp(running[-1])[:, None, None] * carried + update
    return (new_carried, intra + from_state)


def shards(
    ssm_input,
    gate_input,
    b_rows,
    c_rows,
    step_raw,
    step_bias,
    rate_log,
    skip_gain,
    norm_gain,
    w_out,
    residual,
    moe_gain,
    router,
    expert_ids,
    w_gate,
    w_up,
    w_down,
):
    tokens_here = ssm_input.shape[0]
    inner = ssm_input.shape[1]
    heads = rate_log.shape[0]
    head_width = inner // heads
    state_width = b_rows.shape[1]
    blocks = tokens_here // GROUP
    step_sizes = jax.nn.softplus(step_raw + step_bias[None, :])
    log_decay = -step_sizes * jnp.exp(rate_log)[None, :]
    inputs = ssm_input.reshape(tokens_here, heads, head_width)
    pieces = (
        inputs.reshape(blocks, GROUP, heads, head_width),
        b_rows.reshape(blocks, GROUP, state_width),
        c_rows.reshape(blocks, GROUP, state_width),
        step_sizes.reshape(blocks, GROUP, heads),
        log_decay.reshape(blocks, GROUP, heads),
    )
    start = jnp.zeros((heads, head_width, state_width), jnp.float32)
    segment_state, outputs = lax.scan(group_pass, start, pieces)
    slab_log = jnp.cumsum(log_decay, axis=0)
    slab_total = slab_log[-1]
    n_seq = lax.axis_size("seq")
    per_chunk = heads // n_seq
    chunk_rows = per_chunk * head_width
    state_rows = segment_state.reshape(n_seq, chunk_rows, state_width)
    total_rows = jnp.broadcast_to(slab_total.reshape(n_seq, per_chunk, 1), (n_seq, per_chunk, state_width))
    total_block = jnp.pad(total_rows, ((0, 0), (0, 8 - per_chunk), (0, 0)))
    packed = jnp.concatenate([state_rows, total_block], axis=1)
    received = lax.all_to_all(packed, "seq", 0, 0, tiled=True)
    slab_states = received[:, :chunk_rows].reshape(n_seq, per_chunk, head_width, state_width)
    slab_totals = received[:, chunk_rows : chunk_rows + per_chunk, 0]
    order = jnp.arange(n_seq)
    between = (order[None, None, :] > order[None, :, None]) & (order[None, None, :] < order[:, None, None])
    span = jnp.sum(jnp.where(between[:, :, :, None], slab_totals[None, None, :, :], 0.0), axis=2)
    earlier = (order[:, None] > order[None, :])[:, :, None]
    carry_weights = jnp.where(earlier, jnp.exp(span), 0.0)
    entering_each = jnp.sum(
        carry_weights[:, :, :, None, None] * slab_states[None], axis=1
    ).reshape(n_seq, chunk_rows, state_width)
    entering = lax.all_to_all(entering_each, "seq", 0, 0, tiled=True).reshape(
        heads, head_width, state_width
    )
    c_wide = c_rows.astype(jnp.float32)
    arriving = jnp.exp(slab_log)[:, :, None] * jnp.einsum(
        "tn,hpn->thp", c_wide, entering, precision=lax.Precision.HIGHEST
    )
    ssm_out = (
        outputs.reshape(tokens_here, heads, head_width)
        + arriving
        + skip_gain[None, :, None] * inputs.astype(jnp.float32)
    )
    gated = ssm_out.reshape(tokens_here, inner) * jax.nn.silu(gate_input.astype(jnp.float32))
    normed = (
        gated
        * lax.rsqrt(jnp.mean(gated * gated, axis=1, keepdims=True) + 1e-05)
        * norm_gain[None, :]
    ).astype(jnp.bfloat16)
    n_batch = lax.axis_size("batch")
    core = lax.axis_index("batch") % 2
    depth = w_out.shape[0] // 2
    with jax.named_scope("wgather"):
        w_rows = lax.all_gather(
            lax.dynamic_slice_in_dim(w_out, core * depth, depth, axis=0), "seq", axis=1, tiled=True
        )
    partners = [(b, b ^ 1) for b in range(n_batch)]
    own_rows = lax.dynamic_slice_in_dim(normed, core * depth, depth, axis=1)
    partner_rows = lax.ppermute(
        lax.dynamic_slice_in_dim(normed, (1 - core) * depth, depth, axis=1), "batch", partners
    )
    both_parts = jnp.dot(
        jnp.concatenate([partner_rows, own_rows], axis=0), w_rows, preferred_element_type=jnp.float32
    )
    partner_part = both_parts[:tokens_here]
    own_part = both_parts[tokens_here:]
    other_part = lax.ppermute(partner_part, "batch", partners)
    mixer_out = (own_part + other_part).astype(jnp.bfloat16)
    hidden = (residual.astype(jnp.float32) + mixer_out.astype(jnp.float32)).astype(jnp.bfloat16)
    hidden_wide = hidden.astype(jnp.float32)
    moe_input = (
        hidden_wide
        * lax.rsqrt(jnp.mean(hidden_wide * hidden_wide, axis=1, keepdims=True) + 1e-05)
        * moe_gain[None, :]
    ).astype(jnp.bfloat16)
    logits = jnp.dot(moe_input, router, preferred_element_type=jnp.float32)
    chosen = jnp.take_along_axis(logits, expert_ids, axis=1)
    powers = jnp.exp(chosen)
    combine = powers / jnp.sum(powers, axis=1, keepdims=True)
    experts_all = lax.axis_size("seq")
    fanout = expert_ids.shape[1]
    capacity = tokens_here * fanout * 3 // (2 * experts_all)
    width = moe_input.shape[1]
    flat_ids = expert_ids.reshape(-1)
    one_hot = (flat_ids[:, None] == jnp.arange(experts_all, dtype=jnp.int32)[None, :]).astype(
        jnp.int32
    )
    running_count = jnp.cumsum(one_hot, axis=0)
    slot_of = jnp.sum(running_count * one_hot, axis=1) - 1
    target = flat_ids * capacity + slot_of
    slots = experts_all * capacity
    target_pairs = target.reshape(tokens_here, fanout)
    slot_ids = jnp.arange(slots, dtype=jnp.int32)
    placing = jnp.zeros((slots, tokens_here), jnp.bool_)
    for k in range(fanout):
        placing = placing | (slot_ids[:, None] == target_pairs[None, :, k])
    departing_state = jnp.dot(
        placing.astype(jnp.bfloat16), moe_input, preferred_element_type=jnp.float32
    ).astype(jnp.bfloat16)
    departing_state = departing_state.reshape(experts_all, capacity, width)
    batch = lax.all_to_all(departing_state, "seq", split_axis=0, concat_axis=0, tiled=True)
    flat_rows = batch.reshape(-1, width)
    hidden_units = w_gate.shape[2]
    both_proj = jnp.dot(
        flat_rows,
        jnp.concatenate([w_gate[0], w_up[0]], axis=1),
        preferred_element_type=jnp.float32,
    )
    gate_part = both_proj[:, :hidden_units]
    up_part = both_proj[:, hidden_units:]
    expert_hidden = (jax.nn.silu(gate_part) * up_part).astype(jnp.bfloat16)
    result = jnp.dot(expert_hidden, w_down[0], preferred_element_type=jnp.float32).astype(
        jnp.bfloat16
    )
    finished = result.reshape(batch.shape)
    returned = lax.all_to_all(finished, "seq", split_axis=0, concat_axis=0, tiled=True).reshape(
        experts_all * capacity, width
    )
    picking = (target_pairs.T.reshape(-1)[:, None] == slot_ids[None, :]).astype(jnp.bfloat16)
    fetched = jnp.dot(picking, returned, preferred_element_type=jnp.float32).reshape(
        fanout, tokens_here, width
    )
    total = hidden_wide
    for k in range(fanout):
        total = total + combine[:, k][:, None] * fetched[k]
    return total.astype(jnp.bfloat16)


def solution(mesh):
    in_specs = (
        P(("batch", "seq"), None),
        P(("batch", "seq"), None),
        P(("batch", "seq"), None),
        P(("batch", "seq"), None),
        P(("batch", "seq"), None),
        P(),
        P(),
        P(),
        P(),
        P(None, "seq"),
        P(("batch", "seq"), None),
        P(),
        P(),
        P(("batch", "seq"), None),
        P("seq", None, None),
        P("seq", None, None),
        P("seq", None, None),
    )
    out_specs = P(("batch", "seq"), None)
    return jax.shard_map(shards, mesh=mesh, in_specs=in_specs, out_specs=out_specs, check_vma=False)
```
